128 devices in a mesh: seq: 16 (over y, x), emb: 8 (over z, core).
Axes of the slice: x: 4, y: 4, z: 4, core: 2. Of those that a mesh axis runs over, the one named last changes fastest.
Arguments:
- source: bfloat16 [32768, 1024], P('seq', 'emb'), may hold values from -6 to 6
- target: bfloat16 [32768, 1024], P('seq', 'emb'), may hold values from -6 to 6
- doc_ids: int32 [32768], replicated, may hold values from 0 to 511, never falling along the last dimension, each value on 1 to 512 neighbouring positions
- offsets: int32 [512], P(('seq', 'emb')), may hold values from -2048 to 2048, as said below
Outputs:
- projected: bfloat16 [32768, 1024], P('seq', 'emb')
- row_mass: float32 [32768], P(('seq', 'emb'))
The draws below stay inside these ranges and needn't reach their ends.
Inputs may be any that keep to these rules, and one draw needn't show every extreme that they name: doc_ids never fall along the sentences. `offsets`: both ends of the range occur in every draw.
All inputs are finite; a program needn't handle non-finite values.
Results may differ from the reference program's by a relative error of at most 0.006.
Values may be sent and summed in bfloat16 or wider, within the bound.
No kernel may reach another device: no remote copies, remote signals or barrier semaphores. Data moves between devices by JAX's collectives and lax.ppermute only.
A program may use at most 128 MiB of HBM per device.

```python
import math
import jax
import jax.numpy as jnp
import numpy as np
from jax import lax

D = 1024
ROWS_DEV = 256
BAND = 2048
OFFSET_BLOCK = 64
ITERS = 3
SENTENCES = 32768
DOCS = 512


def draw_offsets(key, part):
    count = SENTENCES // OFFSET_BLOCK
    base = jax.random.randint(jax.random.fold_in(key, 11), (count,), -BAND, BAND + 1, dtype=jnp.int32)
    picks = jax.random.permutation(jax.random.fold_in(key, 12), count)
    base = base.at[picks[0]].set(BAND)
    base = base.at[picks[1]].set(-BAND)
    return base.astype(jnp.int32)


def steps_of(key, dims, split, smallest, top_value):
    def one(axis_at, shards_of):
        heights = jax.random.uniform(jax.random.fold_in(jax.random.fold_in(key, 6), axis_at), (shards_of,), jnp.float32, smallest / len(split), top_value / len(split))
        return jnp.repeat(jnp.exp(heights), dims[axis_at] // shards_of).reshape((-1,) + (1,) * (len(dims) - axis_at - 1))

    gain = one(*split[0])
    for cut in split[1:]:
        gain = gain * one(*cut)
    return gain


def profile(count, total, most, skew):
    loads = [(1 << 20) // math.isqrt(standing ** skew) + 1 for standing in range(2, count + 1)]
    spare, holding = total - most - (count - 1), [1] * (count - 1)
    while spare > 0:
        free = [i for i in range(count - 1) if holding[i] < most]
        mass, budget = sum([loads[i] for i in free]), spare
        for i in free:
            addition = min(most - holding[i], max(1, budget * loads[i] // mass), spare)
            holding[i] = holding[i] + addition
            spare = spare - addition
    return np.array([most] + holding)


def uneven_parts(stream_key, number_of, total, bound, slope):
    if number_of == 2:
        one = jax.random.randint(stream_key, (), max(1, total - bound), min(bound, total - 1) + 1)
        return jnp.stack([one, total - one])
    lengths = jnp.asarray(profile(number_of, total, bound, slope), jnp.int32)
    pairs = (number_of - 1) // 2
    donor, receiver = lengths[1:1 + 2 * pairs:2], lengths[2:2 + 2 * pairs:2]
    slack = jnp.minimum(donor - 1, bound - receiver)
    passed = jax.random.randint(jax.random.fold_in(stream_key, 1), (pairs,), 0, 1 << 20) % (slack + 1)
    lengths = lengths.at[1:1 + 2 * pairs:2].set(donor - passed).at[2:2 + 2 * pairs:2].set(receiver + passed)
    return lengths[jax.random.permutation(jax.random.fold_in(stream_key, 2), number_of)]


def gaussian(rng, shape, deviation, most, pieces=(), held_as=jnp.bfloat16):
    result = deviation * jax.random.normal(rng, shape, jnp.float32)
    if pieces:
        result = result * steps_of(rng, shape, pieces, -0.22, 0.18)
    return jnp.clip(result, -most, most).astype(held_as)


def setup_inputs(seed: int = 0) -> dict:
    streams_of = jax.random.split(jax.random.key(seed), 5)
    return {
        "source": gaussian(streams_of[0], (SENTENCES, D), 1.0, 6.0, ((0, 16), (1, 8))),
        "target": gaussian(streams_of[1], (SENTENCES, D), 1.0, 6.0, ((0, 16), (1, 8))),
        "doc_ids": jnp.searchsorted(jnp.cumsum(uneven_parts(streams_of[2], DOCS, SENTENCES, min(512, SENTENCES // 2), 0)), jnp.arange(SENTENCES), side="right").astype(jnp.int32),
        "offsets": draw_offsets(jax.random.fold_in(streams_of[4], 71), 0),
    }


INV_EPS = 50.0
PENALTY = 0.04

def kernel_blocks(source, target, doc_ids, offsets):
    reach = 2 * BAND
    width = ROWS_DEV + 2 * reach
    blocks = SENTENCES // ROWS_DEV
    src_scale = lax.rsqrt(lax.optimization_barrier(jnp.sum(jnp.square(source.astype(jnp.float32)), axis=1)) + 1e-06)
    tgt_scale = lax.rsqrt(lax.optimization_barrier(jnp.sum(jnp.square(target.astype(jnp.float32)), axis=1)) + 1e-06)
    pad_target = jnp.pad(target, ((reach, reach), (0, 0)))
    pad_scale = jnp.pad(tgt_scale, (reach, reach))
    pad_docs = jnp.pad(doc_ids, (reach, reach), constant_values=-1)
    row_offsets = jnp.repeat(offsets, OFFSET_BLOCK)

    def one_block(index):
        start = (index * ROWS_DEV).astype(jnp.int32)
        rows = lax.dynamic_slice_in_dim(source, start, ROWS_DEV, 0)
        window = lax.dynamic_slice_in_dim(pad_target, start, width, 0)
        dots = lax.dot_general(rows, window, (((1,), (1,)), ((), ())), preferred_element_type=jnp.float32)
        cosine = dots * lax.dynamic_slice_in_dim(src_scale, start, ROWS_DEV, 0)[:, None] * lax.dynamic_slice_in_dim(pad_scale, start, width, 0)[None, :]
        src_pos = start + jnp.arange(ROWS_DEV, dtype=jnp.int32)
        tgt_pos = start - reach + jnp.arange(width, dtype=jnp.int32)
        shifted = lax.dynamic_slice_in_dim(row_offsets, start, ROWS_DEV, 0)
        band = (jnp.abs(tgt_pos[None, :] - src_pos[:, None] - shifted[:, None]) <= BAND) & (tgt_pos[None, :] >= 0) & (tgt_pos[None, :] < SENTENCES)
        same = lax.dynamic_slice_in_dim(doc_ids, start, ROWS_DEV, 0)[:, None] == lax.dynamic_slice_in_dim(pad_docs, start, width, 0)[None, :]
        logits = (cosine - jnp.where(same, 0.0, PENALTY)) * INV_EPS
        return jnp.where(band, jnp.exp(logits), 0.0).astype(jnp.float32)
    return lax.map(one_block, jnp.arange(blocks, dtype=jnp.int32))

def reference(source, target, doc_ids, offsets):
    reach = 2 * BAND
    width = ROWS_DEV + 2 * reach
    blocks = SENTENCES // ROWS_DEV
    kernels = kernel_blocks(source, target, doc_ids, offsets)
    starts = jnp.arange(blocks, dtype=jnp.int32) * ROWS_DEV
    pad_scaling = jnp.pad(jnp.ones((SENTENCES,), jnp.float32), (reach, reach))

    def row_sums(scaling):

        def one_row(item):
            kern, start = item
            return lax.optimization_barrier(jnp.sum(kern * lax.dynamic_slice_in_dim(scaling, start, width, 0)[None, :], axis=1))
        return lax.map(one_row, (kernels, starts))

    def add_cols(carry, item):
        kern, weight, start = item
        part = lax.optimization_barrier(jnp.sum(kern * weight[:, None], axis=0))
        current = lax.dynamic_slice_in_dim(carry, start, width, 0)
        return (lax.dynamic_update_slice_in_dim(carry, current + part, start, 0), None)
    inverse = jnp.zeros((blocks, ROWS_DEV), jnp.float32)
    for step in range(ITERS):
        inverse = 1.0 / row_sums(pad_scaling)
        columns, _ = lax.scan(add_cols, jnp.zeros((SENTENCES + 2 * reach,), jnp.float32), (kernels, inverse, starts))
        pad_scaling = jnp.pad(1.0 / columns[reach:reach + SENTENCES], (reach, reach))
    final = row_sums(pad_scaling)
    row_mass = (inverse * final).reshape(SENTENCES)
    pad_target = jnp.pad(target, ((reach, reach), (0, 0)))

    def mix(item):
        kern, totals, start = item
        weights = (kern * lax.dynamic_slice_in_dim(pad_scaling, start, width, 0)[None, :] / totals[:, None]).astype(jnp.bfloat16)
        window = lax.dynamic_slice_in_dim(pad_target, start, width, 0)
        return jnp.dot(weights, window, preferred_element_type=jnp.float32).astype(jnp.bfloat16)
    projected = lax.map(mix, (kernels, final, starts)).reshape(SENTENCES, D)
    return (projected, row_mass)
```

```python
import jax
import jax.numpy as jnp
from jax import lax
from jax.sharding import PartitionSpec as P

BAND = 2048
OFFSET_BLOCK = 64
ITERS = 3


INV_EPS = 50.0
PENALTY = 0.04


def shifted_2(block, axis, distance):
    devices = range(lax.axis_size(axis))
    route = [(i - distance, i) for i in devices if i - distance in devices]
    return lax.ppermute(block, axis, route)


def per_device(source, target, doc_ids, offsets):
    n_emb = lax.axis_size("emb")
    rows_dev = source.shape[0] // n_emb
    place = lax.axis_index(("seq", "emb"))
    sentences = doc_ids.shape[0]
    reach = 2 * BAND
    hops = reach // rows_dev
    width = rows_dev + 2 * reach
    src_rows, tgt_rows = (
        lax.all_to_all(source, "emb", split_axis=0, concat_axis=1, tiled=True),
        lax.all_to_all(target, "emb", split_axis=0, concat_axis=1, tiled=True),
    )
    lower = {}
    upper = {}
    for dist in range(1, hops + 1):
        for sign in (1, -1):
            moved = shifted_2(tgt_rows, ("seq", "emb"), -sign * dist)
            if sign > 0:
                upper[dist] = moved
            else:
                lower[dist] = moved
    pieces = (
        [lower[dist] for dist in range(hops, 0, -1)]
        + [tgt_rows]
        + [upper[dist] for dist in range(1, hops + 1)]
    )
    window = jnp.concatenate(pieces, axis=0)
    src_scale = lax.rsqrt(jnp.sum(jnp.square(src_rows.astype(jnp.float32)), axis=1) + 1e-06)
    tgt_scale = lax.rsqrt(jnp.sum(jnp.square(window.astype(jnp.float32)), axis=1) + 1e-06)
    first_row = place * rows_dev
    src_pos = first_row + jnp.arange(rows_dev, dtype=jnp.int32)
    tgt_pos = first_row - reach + jnp.arange(width, dtype=jnp.int32)
    valid = (tgt_pos >= 0) & (tgt_pos < sentences)
    shifted = jnp.repeat(offsets, OFFSET_BLOCK)
    band = (jnp.abs(tgt_pos[None, :] - src_pos[:, None] - shifted[:, None]) <= BAND) & valid[
        None, :
    ]
    pad_docs = jnp.pad(doc_ids, (reach, reach), constant_values=-1)
    same = (
        lax.dynamic_slice_in_dim(doc_ids, first_row, rows_dev, 0)[:, None]
        == lax.dynamic_slice_in_dim(pad_docs, first_row, width, 0)[None, :]
    )
    penalty = jnp.where(same, 0.0, PENALTY)

    def cosines():
        dots = lax.dot_general(
            src_rows, window, (((1,), (1,)), ((), ())), preferred_element_type=jnp.float32
        )
        return dots * src_scale[:, None] * tgt_scale[None, :]

    def to_kernel(cosine):
        return jnp.where(band, jnp.exp((cosine - penalty) * INV_EPS), 0.0)

    def kernel():
        return to_kernel(cosines())

    padded_len = sentences + 2 * reach

    def column_scaling(part):
        full = lax.dynamic_update_slice_in_dim(
            jnp.zeros((padded_len,), jnp.float32), part, first_row, 0
        )
        columns = lax.psum(full, ("seq", "emb"))
        mine = lax.dynamic_slice_in_dim(columns, first_row, width, 0)
        return jnp.where(valid, 1.0 / jnp.where(valid, mine, 1.0), 0.0)

    scaling = valid.astype(jnp.float32)
    inverse = jnp.zeros((rows_dev,), jnp.float32)
    for step in range(ITERS):
        kern = kernel()
        inverse = 1.0 / jnp.sum(kern * scaling[None, :], axis=1)
        part = jnp.sum(kern * inverse[:, None], axis=0)
        scaling = column_scaling(part)
    kern = kernel()
    totals = jnp.sum(kern * scaling[None, :], axis=1)
    row_mass = inverse * totals
    weights = (kern * scaling[None, :] / totals[:, None]).astype(jnp.bfloat16)
    mixed = jnp.dot(weights, window, preferred_element_type=jnp.float32).astype(jnp.bfloat16)
    projected = lax.all_to_all(mixed, "emb", split_axis=1, concat_axis=0, tiled=True)
    return (projected, row_mass)


def solution(mesh):
    in_specs = (P("seq", "emb"), P("seq", "emb"), P(), P(("seq", "emb")))
    out_specs = (P("seq", "emb"), P(("seq", "emb")))
    return jax.shard_map(
        per_device, mesh=mesh, in_specs=in_specs, out_specs=out_specs, check_vma=False
    )
```

```python
import jax
import jax.numpy as jnp
from jax import lax
from jax.sharding import PartitionSpec as P

BAND = 2048
OFFSET_BLOCK = 64
ITERS = 3


INV_EPS = 50.0
PENALTY = 0.04


def shifted_2(block, axis, distance):
    devices = range(lax.axis_size(axis))
    route = [(i - distance, i) for i in devices if i - distance in devices]
    return lax.ppermute(block, axis, route)


def per_device(source, target, doc_ids, offsets):
    n_emb = lax.axis_size("emb")
    rows_dev = source.shape[0] // n_emb
    place = lax.axis_index(("seq", "emb"))
    sentences = doc_ids.shape[0]
    reach = 2 * BAND
    hops = reach // rows_dev
    width = rows_dev + 2 * reach
    src_rows, tgt_rows = (
        lax.all_to_all(source, "emb", split_axis=0, concat_axis=1, tiled=True),
        lax.all_to_all(target, "emb", split_axis=0, concat_axis=1, tiled=True),
    )
    lower = {}
    upper = {}
    for dist in range(1, hops + 1):
        for sign in (1, -1):
            moved = shifted_2(tgt_rows, ("seq", "emb"), -sign * dist)
            if sign > 0:
                upper[dist] = moved
            else:
                lower[dist] = moved
    pieces = (
        [lower[dist] for dist in range(hops, 0, -1)]
        + [tgt_rows]
        + [upper[dist] for dist in range(1, hops + 1)]
    )
    window = jnp.concatenate(pieces, axis=0)
    src_scale = lax.rsqrt(jnp.sum(jnp.square(src_rows.astype(jnp.float32)), axis=1) + 1e-06)
    tgt_scale = lax.rsqrt(jnp.sum(jnp.square(window.astype(jnp.float32)), axis=1) + 1e-06)
    first_row = place * rows_dev
    src_pos = first_row + jnp.arange(rows_dev, dtype=jnp.int32)
    tgt_pos = first_row - reach + jnp.arange(width, dtype=jnp.int32)
    valid = (tgt_pos >= 0) & (tgt_pos < sentences)
    shifted = jnp.repeat(offsets, OFFSET_BLOCK)
    band = (jnp.abs(tgt_pos[None, :] - src_pos[:, None] - shifted[:, None]) <= BAND) & valid[
        None, :
    ]
    pad_docs = jnp.pad(doc_ids, (reach, reach), constant_values=-1)
    same = (
        lax.dynamic_slice_in_dim(doc_ids, first_row, rows_dev, 0)[:, None]
        == lax.dynamic_slice_in_dim(pad_docs, first_row, width, 0)[None, :]
    )
    penalty = jnp.where(same, 0.0, PENALTY)

    def cosines():
        dots = lax.dot_general(
            src_rows, window, (((1,), (1,)), ((), ())), preferred_element_type=jnp.float32
        )
        return dots * src_scale[:, None] * tgt_scale[None, :]

    def to_kernel(cosine):
        return jnp.where(band, jnp.exp((cosine - penalty) * INV_EPS), 0.0)

    def kernel():
        return to_kernel(cosines())

    n_emb_axis = lax.axis_size("emb")
    block_rows = rows_dev * n_emb_axis
    span = block_rows + 2 * reach
    emb_index = lax.axis_index("emb")
    seq_hops = reach // block_rows

    def emb_sum(x):
        step = 1
        while step < n_emb_axis:
            route = [(e, e ^ step) for e in range(n_emb_axis)]
            x = x + lax.ppermute(x, "emb", route)
            step *= 2
        return x

    def column_scaling(part):
        block = lax.dynamic_update_slice_in_dim(
            jnp.zeros((span,), jnp.float32), part, emb_index * rows_dev, 0
        )
        block = emb_sum(block)
        total = block
        for d in range(1, 2 * seq_hops + 1):
            keep = span - d * block_rows
            upper = shifted_2(block[:keep], "seq", -d)
            lower = shifted_2(block[d * block_rows :], "seq", d)
            total = total + jnp.pad(upper, (d * block_rows, 0)) + jnp.pad(lower, (0, d * block_rows))
        mine = lax.dynamic_slice_in_dim(total, emb_index * rows_dev, width, 0)
        return jnp.where(valid, 1.0 / jnp.where(valid, mine, 1.0), 0.0)

    scaling = valid.astype(jnp.float32)
    inverse = jnp.zeros((rows_dev,), jnp.float32)
    for step in range(ITERS):
        kern = kernel()
        inverse = 1.0 / jnp.sum(kern * scaling[None, :], axis=1)
        part = jnp.sum(kern * inverse[:, None], axis=0)
        scaling = column_scaling(part)
    kern = kernel()
    totals = jnp.sum(kern * scaling[None, :], axis=1)
    row_mass = inverse * totals
    weights = (kern * scaling[None, :] / totals[:, None]).astype(jnp.bfloat16)
    mixed = jnp.dot(weights, window, preferred_element_type=jnp.float32).astype(jnp.bfloat16)
    projected = lax.all_to_all(mixed, "emb", split_axis=1, concat_axis=0, tiled=True)
    return (projected, row_mass)


def solution(mesh):
    in_specs = (P("seq", "emb"), P("seq", "emb"), P(), P(("seq", "emb")))
    out_specs = (P("seq", "emb"), P(("seq", "emb")))
    return jax.shard_map(
        per_device, mesh=mesh, in_specs=in_specs, out_specs=out_specs, check_vma=False
    )
```

```python
import jax
import jax.numpy as jnp
from jax import lax
from jax.sharding import PartitionSpec as P

BAND = 2048
OFFSET_BLOCK = 64
ITERS = 3


INV_EPS = 50.0
PENALTY = 0.04


def shifted_2(block, axis, distance):
    devices = range(lax.axis_size(axis))
    route = [(i - distance, i) for i in devices if i - distance in devices]
    return lax.ppermute(block, axis, route)


def per_device(source, target, doc_ids, offsets):
    n_emb = lax.axis_size("emb")
    rows_dev = source.shape[0] // n_emb
    place = lax.axis_index(("seq", "emb"))
    sentences = doc_ids.shape[0]
    reach = 2 * BAND
    hops = reach // rows_dev
    width = rows_dev + 2 * reach
    src_rows, tgt_rows = (
        lax.all_to_all(source, "emb", split_axis=0, concat_axis=1, tiled=True),
        lax.all_to_all(target, "emb", split_axis=0, concat_axis=1, tiled=True),
    )
    half = hops // 2
    core = place % 2
    fetched = []
    for m in range(-half, half + 1):
        if m == 0:
            fetched.append(tgt_rows)
        else:
            fetched.append(shifted_2(tgt_rows, ("seq", "emb"), -2 * m))
    own = jnp.concatenate(fetched, axis=0)
    n_emb_axis = lax.axis_size("emb")
    peer = lax.ppermute(own, "emb", [(e, e ^ 1) for e in range(n_emb_axis)])
    window = jnp.concatenate([own, peer], axis=0)
    slots = 2 * half + 1
    lag = 2 * (jnp.arange(slots, dtype=jnp.int32) - half)
    slot_chunk = jnp.concatenate([place + lag, place + (1 - 2 * core) + lag])
    src_scale = lax.rsqrt(jnp.sum(jnp.square(src_rows.astype(jnp.float32)), axis=1) + 1e-06)
    tgt_scale = lax.rsqrt(jnp.sum(jnp.square(window.astype(jnp.float32)), axis=1) + 1e-06)
    first_row = place * rows_dev
    src_pos = first_row + jnp.arange(rows_dev, dtype=jnp.int32)
    tgt_pos = (slot_chunk[:, None] * rows_dev + jnp.arange(rows_dev, dtype=jnp.int32)[None, :]).reshape(-1)
    valid = (tgt_pos >= 0) & (tgt_pos < sentences)
    shifted = jnp.repeat(offsets, OFFSET_BLOCK)
    band = (jnp.abs(tgt_pos[None, :] - src_pos[:, None] - shifted[:, None]) <= BAND) & valid[
        None, :
    ]
    pad_docs = jnp.pad(doc_ids, (reach, reach), constant_values=-1)
    same = (
        lax.dynamic_slice_in_dim(doc_ids, first_row, rows_dev, 0)[:, None]
        == jnp.take(pad_docs, jnp.clip(tgt_pos + reach, 0, sentences + 2 * reach - 1))[None, :]
    )
    penalty = jnp.where(same, 0.0, PENALTY)

    def cosines():
        dots = lax.dot_general(
            src_rows, window, (((1,), (1,)), ((), ())), preferred_element_type=jnp.float32
        )
        return dots * src_scale[:, None] * tgt_scale[None, :]

    def to_kernel(cosine):
        return jnp.where(band, jnp.exp((cosine - penalty) * INV_EPS), 0.0)

    def kernel():
        return to_kernel(cosines())

    block_rows = rows_dev * n_emb_axis
    span = block_rows + 2 * reach
    emb_index = lax.axis_index("emb")
    seq_hops = reach // block_rows

    def emb_sum(x):
        step = 1
        while step < n_emb_axis:
            route = [(e, e ^ step) for e in range(n_emb_axis)]
            x = x + lax.ppermute(x, "emb", route)
            step *= 2
        return x

    def column_scaling(part):
        own_p, peer_p = part.reshape(2, slots, rows_dev)
        first = jnp.where(core == 0, own_p, peer_p)
        second = jnp.where(core == 0, peer_p, own_p)
        woven = jnp.stack([first, second], axis=1).reshape(-1)
        block = lax.dynamic_update_slice_in_dim(
            jnp.zeros((span,), jnp.float32), woven, (emb_index - core) * rows_dev, 0
        )
        block = emb_sum(block)
        total = block
        for d in range(1, 2 * seq_hops + 1):
            keep = span - d * block_rows
            upper = shifted_2(block[:keep], "seq", -d)
            lower = shifted_2(block[d * block_rows :], "seq", d)
            total = total + jnp.pad(upper, (d * block_rows, 0)) + jnp.pad(lower, (0, d * block_rows))
        mine = lax.dynamic_slice_in_dim(total, (emb_index - core) * rows_dev, 2 * slots * rows_dev, 0)
        mine = mine.reshape(slots, 2, rows_dev)
        first, second = mine[:, 0], mine[:, 1]
        own_s = jnp.where(core == 0, first, second)
        peer_s = jnp.where(core == 0, second, first)
        cols = jnp.concatenate([own_s, peer_s]).reshape(-1)
        return jnp.where(valid, 1.0 / jnp.where(valid, cols, 1.0), 0.0)

    scaling = valid.astype(jnp.float32)
    inverse = jnp.zeros((rows_dev,), jnp.float32)
    for step in range(ITERS):
        kern = kernel()
        inverse = 1.0 / jnp.sum(kern * scaling[None, :], axis=1)
        part = jnp.sum(kern * inverse[:, None], axis=0)
        scaling = column_scaling(part)
    kern = kernel()
    totals = jnp.sum(kern * scaling[None, :], axis=1)
    row_mass = inverse * totals
    weights = (kern * scaling[None, :] / totals[:, None]).astype(jnp.bfloat16)
    mixed = jnp.dot(weights, window, preferred_element_type=jnp.float32).astype(jnp.bfloat16)
    projected = lax.all_to_all(mixed, "emb", split_axis=1, concat_axis=0, tiled=True)
    return (projected, row_mass)


def solution(mesh):
    in_specs = (P("seq", "emb"), P("seq", "emb"), P(), P(("seq", "emb")))
    out_specs = (P("seq", "emb"), P(("seq", "emb")))
    return jax.shard_map(
        per_device, mesh=mesh, in_specs=in_specs, out_specs=out_specs, check_vma=False
    )
```

```python
import jax
import jax.numpy as jnp
from jax import lax
from jax.sharding import PartitionSpec as P

BAND = 2048
OFFSET_BLOCK = 64
ITERS = 3


INV_EPS = 50.0
PENALTY = 0.04


def shifted_2(block, axis, distance):
    devices = range(lax.axis_size(axis))
    route = [(i - distance, i) for i in devices if i - distance in devices]
    return lax.ppermute(block, axis, route)


def per_device(source, target, doc_ids, offsets):
    n_emb = lax.axis_size("emb")
    rows_dev = source.shape[0] // n_emb
    place = lax.axis_index(("seq", "emb"))
    sentences = doc_ids.shape[0]
    reach = 2 * BAND
    hops = reach // rows_dev
    width = rows_dev + 2 * reach
    both = lax.all_to_all(
        jnp.stack([source, target]), "emb", split_axis=1, concat_axis=2, tiled=True
    )
    src_rows, tgt_rows = both[0], both[1]
    half = hops // 2
    core = place % 2
    fetched = []
    for m in range(-half, half + 1):
        if m == 0:
            fetched.append(tgt_rows)
        else:
            fetched.append(shifted_2(tgt_rows, ("seq", "emb"), -2 * m))
    own = jnp.concatenate(fetched, axis=0)
    n_emb_axis = lax.axis_size("emb")
    peer = lax.ppermute(own, "emb", [(e, e ^ 1) for e in range(n_emb_axis)])
    window = jnp.concatenate([own, peer], axis=0)
    slots = 2 * half + 1
    lag = 2 * (jnp.arange(slots, dtype=jnp.int32) - half)
    slot_chunk = jnp.concatenate([place + lag, place + (1 - 2 * core) + lag])
    src_scale = lax.rsqrt(jnp.sum(jnp.square(src_rows.astype(jnp.float32)), axis=1) + 1e-06)
    tgt_scale = lax.rsqrt(jnp.sum(jnp.square(window.astype(jnp.float32)), axis=1) + 1e-06)
    first_row = place * rows_dev
    src_pos = first_row + jnp.arange(rows_dev, dtype=jnp.int32)
    tgt_pos = (slot_chunk[:, None] * rows_dev + jnp.arange(rows_dev, dtype=jnp.int32)[None, :]).reshape(-1)
    valid = (tgt_pos >= 0) & (tgt_pos < sentences)
    shifted = jnp.repeat(offsets, OFFSET_BLOCK)
    band = (jnp.abs(tgt_pos[None, :] - src_pos[:, None] - shifted[:, None]) <= BAND) & valid[
        None, :
    ]
    pad_docs = jnp.pad(doc_ids, (reach + rows_dev, reach + rows_dev), constant_values=-1)
    natural = lax.dynamic_slice_in_dim(pad_docs, first_row, (2 * slots + 1) * rows_dev, 0)
    natural = natural.reshape(2 * slots + 1, rows_dev)
    own_docs = natural[1::2]
    peer_docs = jnp.where(core == 0, natural[2::2], natural[0 : 2 * slots : 2])
    tgt_docs = jnp.concatenate([own_docs, peer_docs]).reshape(-1)
    same = (
        lax.dynamic_slice_in_dim(doc_ids, first_row, rows_dev, 0)[:, None] == tgt_docs[None, :]
    )
    penalty = jnp.where(same, 0.0, PENALTY)

    def cosines():
        dots = lax.dot_general(
            src_rows, window, (((1,), (1,)), ((), ())), preferred_element_type=jnp.float32
        )
        return dots * src_scale[:, None] * tgt_scale[None, :]

    def to_kernel(cosine):
        return jnp.where(band, jnp.exp((cosine - penalty) * INV_EPS), 0.0)

    def kernel():
        return to_kernel(cosines())

    block_rows = rows_dev * n_emb_axis
    span = block_rows + 2 * reach
    emb_index = lax.axis_index("emb")
    seq_hops = reach // block_rows

    def emb_sum(x):
        step = 1
        while step < n_emb_axis:
            route = [(e, e ^ step) for e in range(n_emb_axis)]
            x = x + lax.ppermute(x, "emb", route)
            step *= 2
        return x

    def column_scaling(part):
        own_p, peer_p = part.reshape(2, slots, rows_dev)
        first = jnp.where(core == 0, own_p, peer_p)
        second = jnp.where(core == 0, peer_p, own_p)
        woven = jnp.stack([first, second], axis=1).reshape(-1)
        block = lax.dynamic_update_slice_in_dim(
            jnp.zeros((span,), jnp.float32), woven, (emb_index - core) * rows_dev, 0
        )
        block = emb_sum(block)
        total = block
        for d in range(1, 2 * seq_hops + 1):
            keep = span - d * block_rows
            upper = shifted_2(block[:keep], "seq", -d)
            lower = shifted_2(block[d * block_rows :], "seq", d)
            total = total + jnp.pad(upper, (d * block_rows, 0)) + jnp.pad(lower, (0, d * block_rows))
        mine = lax.dynamic_slice_in_dim(total, (emb_index - core) * rows_dev, 2 * slots * rows_dev, 0)
        mine = mine.reshape(slots, 2, rows_dev)
        first, second = mine[:, 0], mine[:, 1]
        own_s = jnp.where(core == 0, first, second)
        peer_s = jnp.where(core == 0, second, first)
        cols = jnp.concatenate([own_s, peer_s]).reshape(-1)
        return jnp.where(valid, 1.0 / jnp.where(valid, cols, 1.0), 0.0)

    scaling = valid.astype(jnp.float32)
    inverse = jnp.zeros((rows_dev,), jnp.float32)
    for step in range(ITERS):
        kern = kernel()
        inverse = 1.0 / jnp.sum(kern * scaling[None, :], axis=1)
        part = jnp.sum(kern * inverse[:, None], axis=0)
        scaling = column_scaling(part)
    kern = kernel()
    totals = jnp.sum(kern * scaling[None, :], axis=1)
    row_mass = inverse * totals
    weights = (kern * scaling[None, :] / totals[:, None]).astype(jnp.bfloat16)
    mixed = jnp.dot(weights, window, preferred_element_type=jnp.float32).astype(jnp.bfloat16)
    projected = lax.all_to_all(mixed, "emb", split_axis=1, concat_axis=0, tiled=True)
    return (projected, row_mass)


def solution(mesh):
    in_specs = (P("seq", "emb"), P("seq", "emb"), P(), P(("seq", "emb")))
    out_specs = (P("seq", "emb"), P(("seq", "emb")))
    return jax.shard_map(
        per_device, mesh=mesh, in_specs=in_specs, out_specs=out_specs, check_vma=False
    )
```

```python
import jax
import jax.numpy as jnp
from jax import lax
from jax.sharding import PartitionSpec as P

BAND = 2048
OFFSET_BLOCK = 64
ITERS = 3


INV_EPS = 50.0
PENALTY = 0.04


def shifted_2(block, axis, distance):
    devices = range(lax.axis_size(axis))
    route = [(i - distance, i) for i in devices if i - distance in devices]
    return lax.ppermute(block, axis, route)


def per_device(source, target, doc_ids, offsets):
    n_emb = lax.axis_size("emb")
    rows_dev = source.shape[0] // n_emb
    place = lax.axis_index(("seq", "emb"))
    sentences = doc_ids.shape[0]
    reach = 2 * BAND
    hops = reach // rows_dev
    width = rows_dev + 2 * reach
    both = lax.all_to_all(
        jnp.stack([source, target]), "emb", split_axis=1, concat_axis=2, tiled=True
    )
    src_rows, tgt_rows = both[0], both[1]
    half = hops // 2
    core = place % 2
    fetched = []
    for m in range(-half, half + 1):
        if m == 0:
            fetched.append(tgt_rows)
        else:
            fetched.append(shifted_2(tgt_rows, ("seq", "emb"), -2 * m))
    own = jnp.concatenate(fetched, axis=0)
    n_emb_axis = lax.axis_size("emb")
    peer = lax.ppermute(own, "emb", [(e, e ^ 1) for e in range(n_emb_axis)])
    window = jnp.concatenate([own, peer], axis=0)
    slots = 2 * half + 1
    lag = 2 * (jnp.arange(slots, dtype=jnp.int32) - half)
    slot_chunk = jnp.concatenate([place + lag, place + (1 - 2 * core) + lag])
    src_scale = lax.rsqrt(jnp.sum(jnp.square(src_rows.astype(jnp.float32)), axis=1) + 1e-06)
    tgt_scale = lax.rsqrt(jnp.sum(jnp.square(window.astype(jnp.float32)), axis=1) + 1e-06)
    first_row = place * rows_dev
    src_pos = first_row + jnp.arange(rows_dev, dtype=jnp.int32)
    tgt_pos = (slot_chunk[:, None] * rows_dev + jnp.arange(rows_dev, dtype=jnp.int32)[None, :]).reshape(-1)
    valid = (tgt_pos >= 0) & (tgt_pos < sentences)
    shifted = jnp.repeat(offsets, OFFSET_BLOCK)
    band = (jnp.abs(tgt_pos[None, :] - src_pos[:, None] - shifted[:, None]) <= BAND) & valid[
        None, :
    ]
    pad_docs = jnp.pad(doc_ids, (reach + rows_dev, reach + rows_dev), constant_values=-1)
    natural = lax.dynamic_slice_in_dim(pad_docs, first_row, (2 * slots + 1) * rows_dev, 0)
    natural = natural.reshape(2 * slots + 1, rows_dev)
    own_docs = natural[1::2]
    peer_docs = jnp.where(core == 0, natural[2::2], natural[0 : 2 * slots : 2])
    tgt_docs = jnp.concatenate([own_docs, peer_docs]).reshape(-1)
    same = (
        lax.dynamic_slice_in_dim(doc_ids, first_row, rows_dev, 0)[:, None] == tgt_docs[None, :]
    )
    penalty = jnp.where(same, 0.0, PENALTY)

    def cosines():
        dots = lax.dot_general(
            src_rows, window, (((1,), (1,)), ((), ())), preferred_element_type=jnp.float32
        )
        return dots * src_scale[:, None] * tgt_scale[None, :]

    def to_kernel(cosine):
        return jnp.where(band, jnp.exp((cosine - penalty) * INV_EPS), 0.0)

    def kernel():
        return to_kernel(cosines())

    n_dev = lax.axis_size(("seq", "emb"))
    edge = slots

    def column_scaling(part):
        own_p, peer_p = part.reshape(2, slots, rows_dev)
        first = jnp.where(core == 0, own_p, peer_p)
        second = jnp.where(core == 0, peer_p, own_p)
        woven = jnp.stack([first, second], axis=1).reshape(2 * slots, rows_dev)
        start = place - 2 * half - core + edge
        spread = lax.dynamic_update_slice_in_dim(
            jnp.zeros((n_dev + 2 * edge, rows_dev), jnp.float32), woven, start, 0
        )
        to_owner = lax.all_to_all(spread[edge : edge + n_dev], ("seq", "emb"), 0, 0, tiled=True)
        own_scaling = 1.0 / jnp.sum(to_owner, axis=0)
        everyone = lax.all_to_all(
            jnp.broadcast_to(own_scaling[None, :], (n_dev, rows_dev)), ("seq", "emb"), 0, 0, tiled=True
        )
        everyone = jnp.pad(everyone, ((edge, edge), (0, 0)))
        mine = lax.dynamic_slice_in_dim(everyone, start, 2 * slots, 0).reshape(slots, 2, rows_dev)
        first, second = mine[:, 0], mine[:, 1]
        own_s = jnp.where(core == 0, first, second)
        peer_s = jnp.where(core == 0, second, first)
        cols = jnp.concatenate([own_s, peer_s]).reshape(-1)
        return jnp.where(valid, cols, 0.0)

    scaling = valid.astype(jnp.float32)
    inverse = jnp.zeros((rows_dev,), jnp.float32)
    for step in range(ITERS):
        kern = kernel()
        inverse = 1.0 / jnp.sum(kern * scaling[None, :], axis=1)
        part = jnp.sum(kern * inverse[:, None], axis=0)
        scaling = column_scaling(part)
    kern = kernel()
    totals = jnp.sum(kern * scaling[None, :], axis=1)
    row_mass = inverse * totals
    weights = (kern * scaling[None, :] / totals[:, None]).astype(jnp.bfloat16)
    mixed = jnp.dot(weights, window, preferred_element_type=jnp.float32).astype(jnp.bfloat16)
    projected = lax.all_to_all(mixed, "emb", split_axis=1, concat_axis=0, tiled=True)
    return (projected, row_mass)


def solution(mesh):
    in_specs = (P("seq", "emb"), P("seq", "emb"), P(), P(("seq", "emb")))
    out_specs = (P("seq", "emb"), P(("seq", "emb")))
    return jax.shard_map(
        per_device, mesh=mesh, in_specs=in_specs, out_specs=out_specs, check_vma=False
    )
```

```python
import jax
import jax.numpy as jnp
from jax import lax
from jax.sharding import PartitionSpec as P

BAND = 2048
OFFSET_BLOCK = 64
ITERS = 3


INV_EPS = 50.0
PENALTY = 0.04


def shifted_2(block, axis, distance):
    devices = range(lax.axis_size(axis))
    route = [(i - distance, i) for i in devices if i - distance in devices]
    return lax.ppermute(block, axis, route)


def per_device(source, target, doc_ids, offsets):
    n_emb = lax.axis_size("emb")
    rows_dev = source.shape[0] // n_emb
    place = lax.axis_index(("seq", "emb"))
    sentences = doc_ids.shape[0]
    reach = 2 * BAND
    hops = reach // rows_dev
    width = rows_dev + 2 * reach
    both = lax.all_to_all(
        jnp.stack([source, target]), "emb", split_axis=1, concat_axis=2, tiled=True
    )
    src_rows, tgt_rows = both[0], both[1]
    half = hops // 2
    core = place % 2
    fetched = []
    for m in range(-half, half + 1):
        if m == 0:
            fetched.append(tgt_rows)
        else:
            fetched.append(shifted_2(tgt_rows, ("seq", "emb"), -2 * m))
    own = jnp.concatenate(fetched, axis=0)
    n_emb_axis = lax.axis_size("emb")
    peer = lax.ppermute(own, "emb", [(e, e ^ 1) for e in range(n_emb_axis)])
    slots = 2 * half + 1
    lag = 2 * (jnp.arange(slots, dtype=jnp.int32) - half)
    slot_chunk = jnp.concatenate([place + lag, place + (1 - 2 * core) + lag])
    src_scale = lax.rsqrt(jnp.sum(jnp.square(src_rows.astype(jnp.float32)), axis=1) + 1e-06)
    own_scale = lax.rsqrt(jnp.sum(jnp.square(own.astype(jnp.float32)), axis=1) + 1e-06)
    peer_scale = lax.rsqrt(jnp.sum(jnp.square(peer.astype(jnp.float32)), axis=1) + 1e-06)
    first_row = place * rows_dev
    src_pos = first_row + jnp.arange(rows_dev, dtype=jnp.int32)
    tgt_pos = (slot_chunk[:, None] * rows_dev + jnp.arange(rows_dev, dtype=jnp.int32)[None, :]).reshape(-1)
    valid = (tgt_pos >= 0) & (tgt_pos < sentences)
    shifted = jnp.repeat(offsets, OFFSET_BLOCK)
    band = (jnp.abs(tgt_pos[None, :] - src_pos[:, None] - shifted[:, None]) <= BAND) & valid[
        None, :
    ]
    pad_docs = jnp.pad(doc_ids, (reach + rows_dev, reach + rows_dev), constant_values=-1)
    natural = lax.dynamic_slice_in_dim(pad_docs, first_row, (2 * slots + 1) * rows_dev, 0)
    natural = natural.reshape(2 * slots + 1, rows_dev)
    own_docs = natural[1::2]
    peer_docs = jnp.where(core == 0, natural[2::2], natural[0 : 2 * slots : 2])
    tgt_docs = jnp.concatenate([own_docs, peer_docs]).reshape(-1)
    same = (
        lax.dynamic_slice_in_dim(doc_ids, first_row, rows_dev, 0)[:, None] == tgt_docs[None, :]
    )
    penalty = jnp.where(same, 0.0, PENALTY)

    def cosines():
        def part(block, scale):
            dots = lax.dot_general(
                src_rows, block, (((1,), (1,)), ((), ())), preferred_element_type=jnp.float32
            )
            return dots * src_scale[:, None] * scale[None, :]

        return jnp.concatenate([part(own, own_scale), part(peer, peer_scale)], axis=1)

    def to_kernel(cosine):
        return jnp.where(band, jnp.exp((cosine - penalty) * INV_EPS), 0.0)

    def kernel():
        return to_kernel(cosines())

    n_dev = lax.axis_size(("seq", "emb"))
    edge = slots

    def column_scaling(part):
        own_p, peer_p = part.reshape(2, slots, rows_dev)
        first = jnp.where(core == 0, own_p, peer_p)
        second = jnp.where(core == 0, peer_p, own_p)
        woven = jnp.stack([first, second], axis=1).reshape(2 * slots, rows_dev)
        start = place - 2 * half - core + edge
        spread = lax.dynamic_update_slice_in_dim(
            jnp.zeros((n_dev + 2 * edge, rows_dev), jnp.float32), woven, start, 0
        )
        to_owner = lax.all_to_all(spread[edge : edge + n_dev], ("seq", "emb"), 0, 0, tiled=True)
        own_scaling = 1.0 / jnp.sum(to_owner, axis=0)
        everyone = lax.all_to_all(
            jnp.broadcast_to(own_scaling[None, :], (n_dev, rows_dev)), ("seq", "emb"), 0, 0, tiled=True
        )
        everyone = jnp.pad(everyone, ((edge, edge), (0, 0)))
        mine = lax.dynamic_slice_in_dim(everyone, start, 2 * slots, 0).reshape(slots, 2, rows_dev)
        first, second = mine[:, 0], mine[:, 1]
        own_s = jnp.where(core == 0, first, second)
        peer_s = jnp.where(core == 0, second, first)
        cols = jnp.concatenate([own_s, peer_s]).reshape(-1)
        return jnp.where(valid, cols, 0.0)

    scaling = valid.astype(jnp.float32)
    inverse = jnp.zeros((rows_dev,), jnp.float32)
    kern = kernel()
    for step in range(ITERS):
        inverse = 1.0 / jnp.sum(kern * scaling[None, :], axis=1)
        part = jnp.sum(kern * inverse[:, None], axis=0)
        scaling = column_scaling(part)
    totals = jnp.sum(kern * scaling[None, :], axis=1)
    row_mass = inverse * totals
    weights = (kern * scaling[None, :] / totals[:, None]).astype(jnp.bfloat16)
    split = own.shape[0]
    mixed = (
        jnp.dot(weights[:, :split], own, preferred_element_type=jnp.float32)
        + jnp.dot(weights[:, split:], peer, preferred_element_type=jnp.float32)
    ).astype(jnp.bfloat16)
    projected = lax.all_to_all(mixed, "emb", split_axis=1, concat_axis=0, tiled=True)
    return (projected, row_mass)


def solution(mesh):
    in_specs = (P("seq", "emb"), P("seq", "emb"), P(), P(("seq", "emb")))
    out_specs = (P("seq", "emb"), P(("seq", "emb")))
    return jax.shard_map(
        per_device, mesh=mesh, in_specs=in_specs, out_specs=out_specs, check_vma=False
    )
```

```python
import jax
import jax.numpy as jnp
from jax import lax
from jax.sharding import PartitionSpec as P

BAND = 2048
OFFSET_BLOCK = 64
ITERS = 3


INV_EPS = 50.0
PENALTY = 0.04


def shifted_2(block, axis, distance):
    devices = range(lax.axis_size(axis))
    route = [(i - distance, i) for i in devices if i - distance in devices]
    return lax.ppermute(block, axis, route)


def per_device(source, target, doc_ids, offsets):
    n_emb = lax.axis_size("emb")
    rows_dev = source.shape[0] // n_emb
    place = lax.axis_index(("seq", "emb"))
    sentences = doc_ids.shape[0]
    reach = 2 * BAND
    hops = reach // rows_dev
    width = rows_dev + 2 * reach
    both = lax.all_to_all(
        jnp.stack([source, target]), "emb", split_axis=1, concat_axis=2, tiled=True
    )
    src_rows, tgt_rows = both[0], both[1]
    half = hops // 2
    core = place % 2
    n_emb_axis = lax.axis_size("emb")
    emb_here = lax.axis_index("emb")
    reach_blocks = -(-(half * 2 + n_emb_axis - 1) // n_emb_axis) - 1
    stacked = jnp.stack(
        [
            tgt_rows if q == 0 else shifted_2(tgt_rows, "seq", -q)
            for q in range(-reach_blocks, reach_blocks + 1)
        ]
    )
    by_m = {}
    for e in range(0, n_emb_axis, 2):
        wanted = [m for m in range(-half, half + 1) if (2 * m - e) % n_emb_axis == 0]
        if e == 0:
            for m in wanted:
                by_m[m] = stacked[(2 * m) // n_emb_axis + reach_blocks]
            continue
        dest = (emb_here - e) % n_emb_axis
        picks = [
            lax.dynamic_index_in_dim(
                stacked, (dest + 2 * m) // n_emb_axis + reach_blocks, 0, keepdims=False
            )
            for m in wanted
        ]
        moved = lax.ppermute(
            jnp.stack(picks),
            "emb",
            [(src, (src - e) % n_emb_axis) for src in range(n_emb_axis)],
        )
        for k, m in enumerate(wanted):
            by_m[m] = moved[k]
    own = jnp.concatenate([by_m[m] for m in range(-half, half + 1)], axis=0)
    peer = lax.ppermute(own, "emb", [(e, e ^ 1) for e in range(n_emb_axis)])
    slots = 2 * half + 1
    lag = 2 * (jnp.arange(slots, dtype=jnp.int32) - half)
    slot_chunk = jnp.concatenate([place + lag, place + (1 - 2 * core) + lag])
    src_scale = lax.rsqrt(jnp.sum(jnp.square(src_rows.astype(jnp.float32)), axis=1) + 1e-06)
    own_scale = lax.rsqrt(jnp.sum(jnp.square(own.astype(jnp.float32)), axis=1) + 1e-06)
    peer_scale = lax.rsqrt(jnp.sum(jnp.square(peer.astype(jnp.float32)), axis=1) + 1e-06)
    first_row = place * rows_dev
    src_pos = first_row + jnp.arange(rows_dev, dtype=jnp.int32)
    tgt_pos = (slot_chunk[:, None] * rows_dev + jnp.arange(rows_dev, dtype=jnp.int32)[None, :]).reshape(-1)
    valid = (tgt_pos >= 0) & (tgt_pos < sentences)
    shifted = jnp.repeat(offsets, OFFSET_BLOCK)
    band = (jnp.abs(tgt_pos[None, :] - src_pos[:, None] - shifted[:, None]) <= BAND) & valid[
        None, :
    ]
    pad_docs = jnp.pad(doc_ids, (reach + rows_dev, reach + rows_dev), constant_values=-1)
    natural = lax.dynamic_slice_in_dim(pad_docs, first_row, (2 * slots + 1) * rows_dev, 0)
    natural = natural.reshape(2 * slots + 1, rows_dev)
    own_docs = natural[1::2]
    peer_docs = jnp.where(core == 0, natural[2::2], natural[0 : 2 * slots : 2])
    tgt_docs = jnp.concatenate([own_docs, peer_docs]).reshape(-1)
    same = (
        lax.dynamic_slice_in_dim(doc_ids, first_row, rows_dev, 0)[:, None] == tgt_docs[None, :]
    )
    penalty = jnp.where(same, 0.0, PENALTY)

    def cosines():
        def part(block, scale):
            dots = lax.dot_general(
                src_rows, block, (((1,), (1,)), ((), ())), preferred_element_type=jnp.float32
            )
            return dots * src_scale[:, None] * scale[None, :]

        return jnp.concatenate([part(own, own_scale), part(peer, peer_scale)], axis=1)

    def to_kernel(cosine):
        return jnp.where(band, jnp.exp((cosine - penalty) * INV_EPS), 0.0)

    def kernel():
        return to_kernel(cosines())

    n_dev = lax.axis_size(("seq", "emb"))
    edge = slots

    def column_scaling(part):
        own_p, peer_p = part.reshape(2, slots, rows_dev)
        first = jnp.where(core == 0, own_p, peer_p)
        second = jnp.where(core == 0, peer_p, own_p)
        woven = jnp.stack([first, second], axis=1).reshape(2 * slots, rows_dev)
        start = place - 2 * half - core + edge
        spread = lax.dynamic_update_slice_in_dim(
            jnp.zeros((n_dev + 2 * edge, rows_dev), jnp.float32), woven, start, 0
        )
        to_owner = lax.all_to_all(spread[edge : edge + n_dev], ("seq", "emb"), 0, 0, tiled=True)
        own_scaling = 1.0 / jnp.sum(to_owner, axis=0)
        everyone = lax.all_to_all(
            jnp.broadcast_to(own_scaling[None, :], (n_dev, rows_dev)), ("seq", "emb"), 0, 0, tiled=True
        )
        everyone = jnp.pad(everyone, ((edge, edge), (0, 0)))
        mine = lax.dynamic_slice_in_dim(everyone, start, 2 * slots, 0).reshape(slots, 2, rows_dev)
        first, second = mine[:, 0], mine[:, 1]
        own_s = jnp.where(core == 0, first, second)
        peer_s = jnp.where(core == 0, second, first)
        cols = jnp.concatenate([own_s, peer_s]).reshape(-1)
        return jnp.where(valid, cols, 0.0)

    scaling = valid.astype(jnp.float32)
    inverse = jnp.zeros((rows_dev,), jnp.float32)
    kern = kernel()
    for step in range(ITERS):
        inverse = 1.0 / jnp.sum(kern * scaling[None, :], axis=1)
        part = jnp.sum(kern * inverse[:, None], axis=0)
        scaling = column_scaling(part)
    totals = jnp.sum(kern * scaling[None, :], axis=1)
    row_mass = inverse * totals
    weights = (kern * scaling[None, :] / totals[:, None]).astype(jnp.bfloat16)
    split = own.shape[0]
    mixed = (
        jnp.dot(weights[:, :split], own, preferred_element_type=jnp.float32)
        + jnp.dot(weights[:, split:], peer, preferred_element_type=jnp.float32)
    ).astype(jnp.bfloat16)
    projected = lax.all_to_all(mixed, "emb", split_axis=1, concat_axis=0, tiled=True)
    return (projected, row_mass)


def solution(mesh):
    in_specs = (P("seq", "emb"), P("seq", "emb"), P(), P(("seq", "emb")))
    out_specs = (P("seq", "emb"), P(("seq", "emb")))
    return jax.shard_map(
        per_device, mesh=mesh, in_specs=in_specs, out_specs=out_specs, check_vma=False
    )
```

```python
import jax
import jax.numpy as jnp
from jax import lax
from jax.sharding import PartitionSpec as P

BAND = 2048
OFFSET_BLOCK = 64
ITERS = 3


INV_EPS = 50.0
PENALTY = 0.04


def shifted_2(block, axis, distance):
    devices = range(lax.axis_size(axis))
    route = [(i - distance, i) for i in devices if i - distance in devices]
    return lax.ppermute(block, axis, route)


def per_device(source, target, doc_ids, offsets):
    n_emb = lax.axis_size("emb")
    rows_dev = source.shape[0] // n_emb
    place = lax.axis_index(("seq", "emb"))
    sentences = doc_ids.shape[0]
    reach = 2 * BAND
    hops = reach // rows_dev
    width = rows_dev + 2 * reach
    tgt_rows = lax.all_to_all(target, "emb", split_axis=0, concat_axis=1, tiled=True)
    src_rows = lax.all_to_all(source, "emb", split_axis=0, concat_axis=1, tiled=True)
    half = hops // 2
    core = place % 2
    n_emb_axis = lax.axis_size("emb")
    emb_here = lax.axis_index("emb")
    reach_blocks = -(-(half * 2 + n_emb_axis - 1) // n_emb_axis) - 1
    stacked = jnp.stack(
        [
            tgt_rows if q == 0 else shifted_2(tgt_rows, "seq", -q)
            for q in range(-reach_blocks, reach_blocks + 1)
        ]
    )
    by_m = {}
    for e in range(0, n_emb_axis, 2):
        wanted = [m for m in range(-half, half + 1) if (2 * m - e) % n_emb_axis == 0]
        if e == 0:
            for m in wanted:
                by_m[m] = stacked[(2 * m) // n_emb_axis + reach_blocks]
            continue
        dest = (emb_here - e) % n_emb_axis
        picks = [
            lax.dynamic_index_in_dim(
                stacked, (dest + 2 * m) // n_emb_axis + reach_blocks, 0, keepdims=False
            )
            for m in wanted
        ]
        moved = lax.ppermute(
            jnp.stack(picks),
            "emb",
            [(src, (src - e) % n_emb_axis) for src in range(n_emb_axis)],
        )
        for k, m in enumerate(wanted):
            by_m[m] = moved[k]
    own = jnp.concatenate([by_m[m] for m in range(-half, half + 1)], axis=0)
    peer = lax.ppermute(own, "emb", [(e, e ^ 1) for e in range(n_emb_axis)])
    slots = 2 * half + 1
    lag = 2 * (jnp.arange(slots, dtype=jnp.int32) - half)
    slot_chunk = jnp.concatenate([place + lag, place + (1 - 2 * core) + lag])
    src_scale = lax.rsqrt(jnp.sum(jnp.square(src_rows.astype(jnp.float32)), axis=1) + 1e-06)
    own_scale = lax.rsqrt(jnp.sum(jnp.square(own.astype(jnp.float32)), axis=1) + 1e-06)
    peer_scale = lax.rsqrt(jnp.sum(jnp.square(peer.astype(jnp.float32)), axis=1) + 1e-06)
    first_row = place * rows_dev
    src_pos = first_row + jnp.arange(rows_dev, dtype=jnp.int32)
    tgt_pos = (slot_chunk[:, None] * rows_dev + jnp.arange(rows_dev, dtype=jnp.int32)[None, :]).reshape(-1)
    valid = (tgt_pos >= 0) & (tgt_pos < sentences)
    shifted = jnp.repeat(offsets, OFFSET_BLOCK)
    band = (jnp.abs(tgt_pos[None, :] - src_pos[:, None] - shifted[:, None]) <= BAND) & valid[
        None, :
    ]
    pad_docs = jnp.pad(doc_ids, (reach + rows_dev, reach + rows_dev), constant_values=-1)
    natural = lax.dynamic_slice_in_dim(pad_docs, first_row, (2 * slots + 1) * rows_dev, 0)
    natural = natural.reshape(2 * slots + 1, rows_dev)
    own_docs = natural[1::2]
    peer_docs = jnp.where(core == 0, natural[2::2], natural[0 : 2 * slots : 2])
    tgt_docs = jnp.concatenate([own_docs, peer_docs]).reshape(-1)
    same = (
        lax.dynamic_slice_in_dim(doc_ids, first_row, rows_dev, 0)[:, None] == tgt_docs[None, :]
    )
    penalty = jnp.where(same, 0.0, PENALTY)

    def cosines():
        def part(block, scale):
            dots = lax.dot_general(
                src_rows, block, (((1,), (1,)), ((), ())), preferred_element_type=jnp.float32
            )
            return dots * src_scale[:, None] * scale[None, :]

        return jnp.concatenate([part(own, own_scale), part(peer, peer_scale)], axis=1)

    def to_kernel(cosine):
        return jnp.where(band, jnp.exp((cosine - penalty) * INV_EPS), 0.0)

    def kernel():
        return to_kernel(cosines())

    n_dev = lax.axis_size(("seq", "emb"))
    edge = slots

    def column_scaling(part):
        own_p, peer_p = part.reshape(2, slots, rows_dev)
        first = jnp.where(core == 0, own_p, peer_p)
        second = jnp.where(core == 0, peer_p, own_p)
        woven = jnp.stack([first, second], axis=1).reshape(2 * slots, rows_dev)
        start = place - 2 * half - core + edge
        spread = lax.dynamic_update_slice_in_dim(
            jnp.zeros((n_dev + 2 * edge, rows_dev), jnp.float32), woven, start, 0
        )
        to_owner = lax.all_to_all(spread[edge : edge + n_dev], ("seq", "emb"), 0, 0, tiled=True)
        own_scaling = 1.0 / jnp.sum(to_owner, axis=0)
        everyone = lax.all_to_all(
            jnp.broadcast_to(own_scaling[None, :], (n_dev, rows_dev)), ("seq", "emb"), 0, 0, tiled=True
        )
        everyone = jnp.pad(everyone, ((edge, edge), (0, 0)))
        mine = lax.dynamic_slice_in_dim(everyone, start, 2 * slots, 0).reshape(slots, 2, rows_dev)
        first, second = mine[:, 0], mine[:, 1]
        own_s = jnp.where(core == 0, first, second)
        peer_s = jnp.where(core == 0, second, first)
        cols = jnp.concatenate([own_s, peer_s]).reshape(-1)
        return jnp.where(valid, cols, 0.0)

    scaling = valid.astype(jnp.float32)
    inverse = jnp.zeros((rows_dev,), jnp.float32)
    kern = kernel()
    for step in range(ITERS):
        inverse = 1.0 / jnp.sum(kern * scaling[None, :], axis=1)
        part = jnp.sum(kern * inverse[:, None], axis=0)
        scaling = column_scaling(part)
    totals = jnp.sum(kern * scaling[None, :], axis=1)
    row_mass = inverse * totals
    weights = (kern * scaling[None, :] / totals[:, None]).astype(jnp.bfloat16)
    split = own.shape[0]
    mixed = (
        jnp.dot(weights[:, :split], own, preferred_element_type=jnp.float32)
        + jnp.dot(weights[:, split:], peer, preferred_element_type=jnp.float32)
    ).astype(jnp.bfloat16)
    projected = lax.all_to_all(mixed, "emb", split_axis=1, concat_axis=0, tiled=True)
    return (projected, row_mass)


def solution(mesh):
    in_specs = (P("seq", "emb"), P("seq", "emb"), P(), P(("seq", "emb")))
    out_specs = (P("seq", "emb"), P(("seq", "emb")))
    return jax.shard_map(
        per_device, mesh=mesh, in_specs=in_specs, out_specs=out_specs, check_vma=False
    )
```

```python
import jax
import jax.numpy as jnp
from jax import lax
from jax.sharding import PartitionSpec as P

BAND = 2048
OFFSET_BLOCK = 64
ITERS = 3


INV_EPS = 50.0
PENALTY = 0.04


def shifted_2(block, axis, distance):
    devices = range(lax.axis_size(axis))
    route = [(i - distance, i) for i in devices if i - distance in devices]
    return lax.ppermute(block, axis, route)


def per_device(source, target, doc_ids, offsets):
    n_emb = lax.axis_size("emb")
    rows_dev = source.shape[0] // n_emb
    place = lax.axis_index(("seq", "emb"))
    sentences = doc_ids.shape[0]
    reach = 2 * BAND
    hops = reach // rows_dev
    width = rows_dev + 2 * reach
    tgt_rows = lax.all_to_all(target, "emb", split_axis=0, concat_axis=1, tiled=True)
    src_rows = lax.all_to_all(source, "emb", split_axis=0, concat_axis=1, tiled=True)
    half = hops // 2
    core = place % 2
    n_emb_axis = lax.axis_size("emb")
    emb_here = lax.axis_index("emb")
    reach_blocks = -(-(half * 2 + n_emb_axis - 1) // n_emb_axis) - 1
    stacked = jnp.stack(
        [
            tgt_rows if q == 0 else shifted_2(tgt_rows, "seq", -q)
            for q in range(-reach_blocks, reach_blocks + 1)
        ]
    )
    src_rows, stacked = lax.optimization_barrier((src_rows, stacked))
    by_m = {}
    for e in range(0, n_emb_axis, 2):
        wanted = [m for m in range(-half, half + 1) if (2 * m - e) % n_emb_axis == 0]
        if e == 0:
            for m in wanted:
                by_m[m] = stacked[(2 * m) // n_emb_axis + reach_blocks]
            continue
        dest = (emb_here - e) % n_emb_axis
        picks = [
            lax.dynamic_index_in_dim(
                stacked, (dest + 2 * m) // n_emb_axis + reach_blocks, 0, keepdims=False
            )
            for m in wanted
        ]
        moved = lax.ppermute(
            jnp.stack(picks),
            "emb",
            [(src, (src - e) % n_emb_axis) for src in range(n_emb_axis)],
        )
        for k, m in enumerate(wanted):
            by_m[m] = moved[k]
    own = jnp.concatenate([by_m[m] for m in range(-half, half + 1)], axis=0)
    peer = lax.ppermute(own, "emb", [(e, e ^ 1) for e in range(n_emb_axis)])
    slots = 2 * half + 1
    lag = 2 * (jnp.arange(slots, dtype=jnp.int32) - half)
    slot_chunk = jnp.concatenate([place + lag, place + (1 - 2 * core) + lag])
    src_scale = lax.rsqrt(jnp.sum(jnp.square(src_rows.astype(jnp.float32)), axis=1) + 1e-06)
    own_scale = lax.rsqrt(jnp.sum(jnp.square(own.astype(jnp.float32)), axis=1) + 1e-06)
    peer_scale = lax.rsqrt(jnp.sum(jnp.square(peer.astype(jnp.float32)), axis=1) + 1e-06)
    first_row = place * rows_dev
    src_pos = first_row + jnp.arange(rows_dev, dtype=jnp.int32)
    tgt_pos = (slot_chunk[:, None] * rows_dev + jnp.arange(rows_dev, dtype=jnp.int32)[None, :]).reshape(-1)
    valid = (tgt_pos >= 0) & (tgt_pos < sentences)
    shifted = jnp.repeat(offsets, OFFSET_BLOCK)
    band = (jnp.abs(tgt_pos[None, :] - src_pos[:, None] - shifted[:, None]) <= BAND) & valid[
        None, :
    ]
    pad_docs = jnp.pad(doc_ids, (reach + rows_dev, reach + rows_dev), constant_values=-1)
    natural = lax.dynamic_slice_in_dim(pad_docs, first_row, (2 * slots + 1) * rows_dev, 0)
    natural = natural.reshape(2 * slots + 1, rows_dev)
    own_docs = natural[1::2]
    peer_docs = jnp.where(core == 0, natural[2::2], natural[0 : 2 * slots : 2])
    tgt_docs = jnp.concatenate([own_docs, peer_docs]).reshape(-1)
    same = (
        lax.dynamic_slice_in_dim(doc_ids, first_row, rows_dev, 0)[:, None] == tgt_docs[None, :]
    )
    penalty = jnp.where(same, 0.0, PENALTY)

    def cosines():
        def part(block, scale):
            dots = lax.dot_general(
                src_rows, block, (((1,), (1,)), ((), ())), preferred_element_type=jnp.float32
            )
            return dots * src_scale[:, None] * scale[None, :]

        return jnp.concatenate([part(own, own_scale), part(peer, peer_scale)], axis=1)

    def to_kernel(cosine):
        return jnp.where(band, jnp.exp((cosine - penalty) * INV_EPS), 0.0)

    def kernel():
        return to_kernel(cosines())

    n_dev = lax.axis_size(("seq", "emb"))
    edge = slots

    def column_scaling(part):
        own_p, peer_p = part.reshape(2, slots, rows_dev)
        first = jnp.where(core == 0, own_p, peer_p)
        second = jnp.where(core == 0, peer_p, own_p)
        woven = jnp.stack([first, second], axis=1).reshape(2 * slots, rows_dev)
        start = place - 2 * half - core + edge
        spread = lax.dynamic_update_slice_in_dim(
            jnp.zeros((n_dev + 2 * edge, rows_dev), jnp.float32), woven, start, 0
        )
        to_owner = lax.all_to_all(spread[edge : edge + n_dev], ("seq", "emb"), 0, 0, tiled=True)
        own_scaling = 1.0 / jnp.sum(to_owner, axis=0)
        everyone = lax.all_to_all(
            jnp.broadcast_to(own_scaling[None, :], (n_dev, rows_dev)), ("seq", "emb"), 0, 0, tiled=True
        )
        everyone = jnp.pad(everyone, ((edge, edge), (0, 0)))
        mine = lax.dynamic_slice_in_dim(everyone, start, 2 * slots, 0).reshape(slots, 2, rows_dev)
        first, second = mine[:, 0], mine[:, 1]
        own_s = jnp.where(core == 0, first, second)
        peer_s = jnp.where(core == 0, second, first)
        cols = jnp.concatenate([own_s, peer_s]).reshape(-1)
        return jnp.where(valid, cols, 0.0)

    scaling = valid.astype(jnp.float32)
    inverse = jnp.zeros((rows_dev,), jnp.float32)
    kern = kernel()
    for step in range(ITERS):
        inverse = 1.0 / jnp.sum(kern * scaling[None, :], axis=1)
        part = jnp.sum(kern * inverse[:, None], axis=0)
        scaling = column_scaling(part)
    totals = jnp.sum(kern * scaling[None, :], axis=1)
    row_mass = inverse * totals
    weights = (kern * scaling[None, :] / totals[:, None]).astype(jnp.bfloat16)
    split = own.shape[0]
    mixed = (
        jnp.dot(weights[:, :split], own, preferred_element_type=jnp.float32)
        + jnp.dot(weights[:, split:], peer, preferred_element_type=jnp.float32)
    ).astype(jnp.bfloat16)
    projected = lax.all_to_all(mixed, "emb", split_axis=1, concat_axis=0, tiled=True)
    return (projected, row_mass)


def solution(mesh):
    in_specs = (P("seq", "emb"), P("seq", "emb"), P(), P(("seq", "emb")))
    out_specs = (P("seq", "emb"), P(("seq", "emb")))
    return jax.shard_map(
        per_device, mesh=mesh, in_specs=in_specs, out_specs=out_specs, check_vma=False
    )
```

```python
import jax
import jax.numpy as jnp
from jax import lax
from jax.sharding import PartitionSpec as P

BAND = 2048
OFFSET_BLOCK = 64
ITERS = 3


INV_EPS = 50.0
PENALTY = 0.04


def shifted_2(block, axis, distance):
    devices = range(lax.axis_size(axis))
    route = [(i - distance, i) for i in devices if i - distance in devices]
    return lax.ppermute(block, axis, route)


def per_device(source, target, doc_ids, offsets):
    n_emb = lax.axis_size("emb")
    rows_dev = source.shape[0] // n_emb
    place = lax.axis_index(("seq", "emb"))
    sentences = doc_ids.shape[0]
    reach = 2 * BAND
    hops = reach // rows_dev
    width = rows_dev + 2 * reach
    tgt_rows = lax.all_to_all(target, "emb", split_axis=0, concat_axis=1, tiled=True)
    src_rows = lax.all_to_all(source, "emb", split_axis=0, concat_axis=1, tiled=True)
    half = hops // 2
    core = place % 2
    n_emb_axis = lax.axis_size("emb")
    emb_here = lax.axis_index("emb")
    reach_blocks = -(-(half * 2 + n_emb_axis - 1) // n_emb_axis) - 1
    stacked = jnp.stack(
        [
            tgt_rows if q == 0 else shifted_2(tgt_rows, "seq", -q)
            for q in range(-reach_blocks, reach_blocks + 1)
        ]
    )
    src_rows, stacked = lax.optimization_barrier((src_rows, stacked))
    by_m = {}
    for e in range(0, n_emb_axis, 2):
        wanted = [m for m in range(-half, half + 1) if (2 * m - e) % n_emb_axis == 0]
        if e == 0:
            for m in wanted:
                by_m[m] = stacked[(2 * m) // n_emb_axis + reach_blocks]
            continue
        dest = (emb_here - e) % n_emb_axis
        for m in wanted:
            pick = lax.dynamic_index_in_dim(
                stacked, (dest + 2 * m) // n_emb_axis + reach_blocks, 0, keepdims=False
            )
            by_m[m] = lax.ppermute(
                pick, "emb", [(src, (src - e) % n_emb_axis) for src in range(n_emb_axis)]
            )
    own = jnp.concatenate([by_m[m] for m in range(-half, half + 1)], axis=0)
    peer = lax.ppermute(own, "emb", [(e, e ^ 1) for e in range(n_emb_axis)])
    slots = 2 * half + 1
    lag = 2 * (jnp.arange(slots, dtype=jnp.int32) - half)
    slot_chunk = jnp.concatenate([place + lag, place + (1 - 2 * core) + lag])
    src_scale = lax.rsqrt(jnp.sum(jnp.square(src_rows.astype(jnp.float32)), axis=1) + 1e-06)
    chunk_scale = {
        m: lax.rsqrt(jnp.sum(jnp.square(by_m[m].astype(jnp.float32)), axis=1) + 1e-06)
        for m in by_m
    }
    peer_scale = lax.rsqrt(jnp.sum(jnp.square(peer.astype(jnp.float32)), axis=1) + 1e-06)
    first_row = place * rows_dev
    src_pos = first_row + jnp.arange(rows_dev, dtype=jnp.int32)
    tgt_pos = (slot_chunk[:, None] * rows_dev + jnp.arange(rows_dev, dtype=jnp.int32)[None, :]).reshape(-1)
    valid = (tgt_pos >= 0) & (tgt_pos < sentences)
    shifted = jnp.repeat(offsets, OFFSET_BLOCK)
    band = (jnp.abs(tgt_pos[None, :] - src_pos[:, None] - shifted[:, None]) <= BAND) & valid[
        None, :
    ]
    pad_docs = jnp.pad(doc_ids, (reach + rows_dev, reach + rows_dev), constant_values=-1)
    natural = lax.dynamic_slice_in_dim(pad_docs, first_row, (2 * slots + 1) * rows_dev, 0)
    natural = natural.reshape(2 * slots + 1, rows_dev)
    own_docs = natural[1::2]
    peer_docs = jnp.where(core == 0, natural[2::2], natural[0 : 2 * slots : 2])
    tgt_docs = jnp.concatenate([own_docs, peer_docs]).reshape(-1)
    same = (
        lax.dynamic_slice_in_dim(doc_ids, first_row, rows_dev, 0)[:, None] == tgt_docs[None, :]
    )
    penalty = jnp.where(same, 0.0, PENALTY)

    def cosines():
        def part(block, scale):
            dots = lax.dot_general(
                src_rows, block, (((1,), (1,)), ((), ())), preferred_element_type=jnp.float32
            )
            return dots * src_scale[:, None] * scale[None, :]

        blocks = [part(by_m[m], chunk_scale[m]) for m in range(-half, half + 1)]
        return jnp.concatenate(blocks + [part(peer, peer_scale)], axis=1)

    def to_kernel(cosine):
        return jnp.where(band, jnp.exp((cosine - penalty) * INV_EPS), 0.0)

    def kernel():
        return to_kernel(cosines())

    n_dev = lax.axis_size(("seq", "emb"))
    edge = slots

    def column_scaling(part):
        own_p, peer_p = part.reshape(2, slots, rows_dev)
        first = jnp.where(core == 0, own_p, peer_p)
        second = jnp.where(core == 0, peer_p, own_p)
        woven = jnp.stack([first, second], axis=1).reshape(2 * slots, rows_dev)
        start = place - 2 * half - core + edge
        spread = lax.dynamic_update_slice_in_dim(
            jnp.zeros((n_dev + 2 * edge, rows_dev), jnp.float32), woven, start, 0
        )
        to_owner = lax.all_to_all(spread[edge : edge + n_dev], ("seq", "emb"), 0, 0, tiled=True)
        own_scaling = 1.0 / jnp.sum(to_owner, axis=0)
        everyone = lax.all_to_all(
            jnp.broadcast_to(own_scaling[None, :], (n_dev, rows_dev)), ("seq", "emb"), 0, 0, tiled=True
        )
        everyone = jnp.pad(everyone, ((edge, edge), (0, 0)))
        mine = lax.dynamic_slice_in_dim(everyone, start, 2 * slots, 0).reshape(slots, 2, rows_dev)
        first, second = mine[:, 0], mine[:, 1]
        own_s = jnp.where(core == 0, first, second)
        peer_s = jnp.where(core == 0, second, first)
        cols = jnp.concatenate([own_s, peer_s]).reshape(-1)
        return jnp.where(valid, cols, 0.0)

    scaling = valid.astype(jnp.float32)
    inverse = jnp.zeros((rows_dev,), jnp.float32)
    kern = kernel()
    for step in range(ITERS):
        inverse = 1.0 / jnp.sum(kern * scaling[None, :], axis=1)
        part = jnp.sum(kern * inverse[:, None], axis=0)
        scaling = column_scaling(part)
    totals = jnp.sum(kern * scaling[None, :], axis=1)
    row_mass = inverse * totals
    weights = (kern * scaling[None, :] / totals[:, None]).astype(jnp.bfloat16)
    split = own.shape[0]
    mixed = (
        jnp.dot(weights[:, :split], own, preferred_element_type=jnp.float32)
        + jnp.dot(weights[:, split:], peer, preferred_element_type=jnp.float32)
    ).astype(jnp.bfloat16)
    projected = lax.all_to_all(mixed, "emb", split_axis=1, concat_axis=0, tiled=True)
    return (projected, row_mass)


def solution(mesh):
    in_specs = (P("seq", "emb"), P("seq", "emb"), P(), P(("seq", "emb")))
    out_specs = (P("seq", "emb"), P(("seq", "emb")))
    return jax.shard_map(
        per_device, mesh=mesh, in_specs=in_specs, out_specs=out_specs, check_vma=False
    )
```

```python
import jax
import jax.numpy as jnp
from jax import lax
from jax.sharding import PartitionSpec as P

BAND = 2048
OFFSET_BLOCK = 64
ITERS = 3


INV_EPS = 50.0
PENALTY = 0.04


def shifted_2(block, axis, distance):
    devices = range(lax.axis_size(axis))
    route = [(i - distance, i) for i in devices if i - distance in devices]
    return lax.ppermute(block, axis, route)


def per_device(source, target, doc_ids, offsets):
    n_emb = lax.axis_size("emb")
    rows_dev = source.shape[0] // n_emb
    place = lax.axis_index(("seq", "emb"))
    sentences = doc_ids.shape[0]
    reach = 2 * BAND
    hops = reach // rows_dev
    width = rows_dev + 2 * reach
    tgt_rows = lax.all_to_all(target, "emb", split_axis=0, concat_axis=1, tiled=True)
    src_rows = lax.all_to_all(source, "emb", split_axis=0, concat_axis=1, tiled=True)
    half = hops // 2
    core = place % 2
    n_emb_axis = lax.axis_size("emb")
    emb_here = lax.axis_index("emb")
    reach_blocks = -(-(half * 2 + n_emb_axis - 1) // n_emb_axis) - 1
    stacked = jnp.stack(
        [
            tgt_rows if q == 0 else shifted_2(tgt_rows, "seq", -q)
            for q in range(-reach_blocks, reach_blocks + 1)
        ]
    )
    src_rows, stacked = lax.optimization_barrier((src_rows, stacked))
    by_m = {}
    for e in range(0, n_emb_axis, 2):
        wanted = [m for m in range(-half, half + 1) if (2 * m - e) % n_emb_axis == 0]
        if e == 0:
            for m in wanted:
                by_m[m] = stacked[(2 * m) // n_emb_axis + reach_blocks]
            continue
        dest = (emb_here - e) % n_emb_axis
        picks = [
            lax.dynamic_index_in_dim(
                stacked, (dest + 2 * m) // n_emb_axis + reach_blocks, 0, keepdims=False
            )
            for m in wanted
        ]
        moved = lax.ppermute(
            jnp.stack(picks),
            "emb",
            [(src, (src - e) % n_emb_axis) for src in range(n_emb_axis)],
        )
        for k, m in enumerate(wanted):
            by_m[m] = moved[k]
    own = jnp.concatenate([by_m[m] for m in range(-half, half + 1)], axis=0)
    peer = lax.ppermute(own, "emb", [(e, e ^ 1) for e in range(n_emb_axis)])
    slots = 2 * half + 1
    lag = 2 * (jnp.arange(slots, dtype=jnp.int32) - half)
    slot_chunk = jnp.concatenate([place + lag, place + (1 - 2 * core) + lag])
    src_scale = lax.rsqrt(jnp.sum(jnp.square(src_rows.astype(jnp.float32)), axis=1) + 1e-06)
    own_scale = lax.rsqrt(jnp.sum(jnp.square(own.astype(jnp.float32)), axis=1) + 1e-06)
    peer_scale = lax.ppermute(own_scale, "emb", [(e, e ^ 1) for e in range(n_emb_axis)])
    first_row = place * rows_dev
    src_pos = first_row + jnp.arange(rows_dev, dtype=jnp.int32)
    tgt_pos = (slot_chunk[:, None] * rows_dev + jnp.arange(rows_dev, dtype=jnp.int32)[None, :]).reshape(-1)
    valid = (tgt_pos >= 0) & (tgt_pos < sentences)
    shifted = jnp.repeat(offsets, OFFSET_BLOCK)
    band = (jnp.abs(tgt_pos[None, :] - src_pos[:, None] - shifted[:, None]) <= BAND) & valid[
        None, :
    ]
    pad_docs = jnp.pad(doc_ids, (reach + rows_dev, reach + rows_dev), constant_values=-1)
    natural = lax.dynamic_slice_in_dim(pad_docs, first_row, (2 * slots + 1) * rows_dev, 0)
    natural = natural.reshape(2 * slots + 1, rows_dev)
    own_docs = natural[1::2]
    peer_docs = jnp.where(core == 0, natural[2::2], natural[0 : 2 * slots : 2])
    tgt_docs = jnp.concatenate([own_docs, peer_docs]).reshape(-1)
    same = (
        lax.dynamic_slice_in_dim(doc_ids, first_row, rows_dev, 0)[:, None] == tgt_docs[None, :]
    )
    penalty = jnp.where(same, 0.0, PENALTY)

    def cosines():
        def part(block, scale):
            dots = lax.dot_general(
                src_rows, block, (((1,), (1,)), ((), ())), preferred_element_type=jnp.float32
            )
            return dots * src_scale[:, None] * scale[None, :]

        return jnp.concatenate([part(own, own_scale), part(peer, peer_scale)], axis=1)

    def to_kernel(cosine):
        return jnp.where(band, jnp.exp((cosine - penalty) * INV_EPS), 0.0)

    def kernel():
        return to_kernel(cosines())

    n_dev = lax.axis_size(("seq", "emb"))
    edge = slots

    def column_scaling(part):
        own_p, peer_p = part.reshape(2, slots, rows_dev)
        first = jnp.where(core == 0, own_p, peer_p)
        second = jnp.where(core == 0, peer_p, own_p)
        woven = jnp.stack([first, second], axis=1).reshape(2 * slots, rows_dev)
        start = place - 2 * half - core + edge
        spread = lax.dynamic_update_slice_in_dim(
            jnp.zeros((n_dev + 2 * edge, rows_dev), jnp.float32), woven, start, 0
        )
        to_owner = lax.all_to_all(spread[edge : edge + n_dev], ("seq", "emb"), 0, 0, tiled=True)
        own_scaling = 1.0 / jnp.sum(to_owner, axis=0)
        everyone = lax.all_to_all(
            jnp.broadcast_to(own_scaling[None, :], (n_dev, rows_dev)), ("seq", "emb"), 0, 0, tiled=True
        )
        everyone = jnp.pad(everyone, ((edge, edge), (0, 0)))
        mine = lax.dynamic_slice_in_dim(everyone, start, 2 * slots, 0).reshape(slots, 2, rows_dev)
        first, second = mine[:, 0], mine[:, 1]
        own_s = jnp.where(core == 0, first, second)
        peer_s = jnp.where(core == 0, second, first)
        cols = jnp.concatenate([own_s, peer_s]).reshape(-1)
        return jnp.where(valid, cols, 0.0)

    scaling = valid.astype(jnp.float32)
    inverse = jnp.zeros((rows_dev,), jnp.float32)
    kern = kernel()
    for step in range(ITERS):
        inverse = 1.0 / jnp.sum(kern * scaling[None, :], axis=1)
        part = jnp.sum(kern * inverse[:, None], axis=0)
        scaling = column_scaling(part)
    totals = jnp.sum(kern * scaling[None, :], axis=1)
    row_mass = inverse * totals
    weights = (kern * scaling[None, :] / totals[:, None]).astype(jnp.bfloat16)
    split = own.shape[0]
    mixed = (
        jnp.dot(weights[:, :split], own, preferred_element_type=jnp.float32)
        + jnp.dot(weights[:, split:], peer, preferred_element_type=jnp.float32)
    ).astype(jnp.bfloat16)
    projected = lax.all_to_all(mixed, "emb", split_axis=1, concat_axis=0, tiled=True)
    return (projected, row_mass)


def solution(mesh):
    in_specs = (P("seq", "emb"), P("seq", "emb"), P(), P(("seq", "emb")))
    out_specs = (P("seq", "emb"), P(("seq", "emb")))
    return jax.shard_map(
        per_device, mesh=mesh, in_specs=in_specs, out_specs=out_specs, check_vma=False
    )
```

```python
import jax
import jax.numpy as jnp
from jax import lax
from jax.sharding import PartitionSpec as P

BAND = 2048
OFFSET_BLOCK = 64
ITERS = 3


INV_EPS = 50.0
PENALTY = 0.04


def shifted_2(block, axis, distance):
    devices = range(lax.axis_size(axis))
    route = [(i - distance, i) for i in devices if i - distance in devices]
    return lax.ppermute(block, axis, route)


def per_device(source, target, doc_ids, offsets):
    n_emb = lax.axis_size("emb")
    rows_dev = source.shape[0] // n_emb
    place = lax.axis_index(("seq", "emb"))
    sentences = doc_ids.shape[0]
    reach = 2 * BAND
    hops = reach // rows_dev
    width = rows_dev + 2 * reach
    tgt_rows = lax.all_to_all(target, "emb", split_axis=0, concat_axis=1, tiled=True)
    src_rows = lax.all_to_all(source, "emb", split_axis=0, concat_axis=1, tiled=True)
    half = hops // 2
    core = place % 2
    n_emb_axis = lax.axis_size("emb")
    emb_here = lax.axis_index("emb")
    reach_blocks = -(-(half * 2 + n_emb_axis - 1) // n_emb_axis) - 1
    stacked = jnp.stack(
        [
            tgt_rows if q == 0 else shifted_2(tgt_rows, "seq", -q)
            for q in range(-reach_blocks, reach_blocks + 1)
        ]
    )
    src_rows, stacked = lax.optimization_barrier((src_rows, stacked))
    groups = []
    order = []
    for e in range(0, n_emb_axis, 2):
        wanted = [m for m in range(-half, half + 1) if (2 * m - e) % n_emb_axis == 0]
        order += wanted
        if e == 0:
            groups.append(stacked)
            continue
        dest = (emb_here - e) % n_emb_axis
        picks = [
            lax.dynamic_index_in_dim(
                stacked, (dest + 2 * m) // n_emb_axis + reach_blocks, 0, keepdims=False
            )
            for m in wanted
        ]
        groups.append(
            lax.ppermute(
                jnp.stack(picks),
                "emb",
                [(src, (src - e) % n_emb_axis) for src in range(n_emb_axis)],
            )
        )
    own_groups = [g.reshape(-1, g.shape[-1]) for g in groups]

    def swap(x):
        return lax.ppermute(x, "emb", [(e, e ^ 1) for e in range(n_emb_axis)])

    peer_groups = [swap(g) for g in own_groups]
    slots = 2 * half + 1
    lag = 2 * jnp.asarray(order, dtype=jnp.int32)
    slot_chunk = jnp.concatenate([place + lag, place + (1 - 2 * core) + lag])
    src_scale = lax.rsqrt(jnp.sum(jnp.square(src_rows.astype(jnp.float32)), axis=1) + 1e-06)
    own_scales = [
        lax.rsqrt(jnp.sum(jnp.square(g.astype(jnp.float32)), axis=1) + 1e-06) for g in own_groups
    ]
    peer_scale = swap(jnp.concatenate(own_scales))
    sizes = [g.shape[0] for g in own_groups]
    bounds = [sum(sizes[:k]) for k in range(len(sizes) + 1)]
    peer_scales = [peer_scale[bounds[k] : bounds[k + 1]] for k in range(len(sizes))]
    rank = {m: k for k, m in enumerate(order)}

    def to_m_order(rows):
        return jnp.stack([rows[rank[m]] for m in range(-half, half + 1)])

    def to_slot_order(rows):
        return jnp.stack([rows[m + half] for m in order])

    first_row = place * rows_dev
    src_pos = first_row + jnp.arange(rows_dev, dtype=jnp.int32)
    tgt_pos = (slot_chunk[:, None] * rows_dev + jnp.arange(rows_dev, dtype=jnp.int32)[None, :]).reshape(-1)
    valid = (tgt_pos >= 0) & (tgt_pos < sentences)
    shifted = jnp.repeat(offsets, OFFSET_BLOCK)
    band = (jnp.abs(tgt_pos[None, :] - src_pos[:, None] - shifted[:, None]) <= BAND) & valid[
        None, :
    ]
    pad_docs = jnp.pad(doc_ids, (reach + rows_dev, reach + rows_dev), constant_values=-1)
    natural = lax.dynamic_slice_in_dim(pad_docs, first_row, (2 * slots + 1) * rows_dev, 0)
    natural = natural.reshape(2 * slots + 1, rows_dev)
    own_docs = to_slot_order(natural[1::2])
    peer_docs = to_slot_order(jnp.where(core == 0, natural[2::2], natural[0 : 2 * slots : 2]))
    tgt_docs = jnp.concatenate([own_docs, peer_docs]).reshape(-1)
    same = (
        lax.dynamic_slice_in_dim(doc_ids, first_row, rows_dev, 0)[:, None] == tgt_docs[None, :]
    )
    penalty = jnp.where(same, 0.0, PENALTY)

    def cosines():
        def part(block, scale):
            dots = lax.dot_general(
                src_rows, block, (((1,), (1,)), ((), ())), preferred_element_type=jnp.float32
            )
            return dots * src_scale[:, None] * scale[None, :]

        blocks = [part(g, sc) for g, sc in zip(own_groups, own_scales)]
        blocks += [part(g, sc) for g, sc in zip(peer_groups, peer_scales)]
        return jnp.concatenate(blocks, axis=1)

    def to_kernel(cosine):
        return jnp.where(band, jnp.exp((cosine - penalty) * INV_EPS), 0.0)

    def kernel():
        return to_kernel(cosines())

    n_dev = lax.axis_size(("seq", "emb"))
    edge = slots

    def column_scaling(part):
        own_p, peer_p = part.reshape(2, slots, rows_dev)
        own_p, peer_p = to_m_order(own_p), to_m_order(peer_p)
        first = jnp.where(core == 0, own_p, peer_p)
        second = jnp.where(core == 0, peer_p, own_p)
        woven = jnp.stack([first, second], axis=1).reshape(2 * slots, rows_dev)
        start = place - 2 * half - core + edge
        spread = lax.dynamic_update_slice_in_dim(
            jnp.zeros((n_dev + 2 * edge, rows_dev), jnp.float32), woven, start, 0
        )
        to_owner = lax.all_to_all(spread[edge : edge + n_dev], ("seq", "emb"), 0, 0, tiled=True)
        own_scaling = 1.0 / jnp.sum(to_owner, axis=0)
        everyone = lax.all_to_all(
            jnp.broadcast_to(own_scaling[None, :], (n_dev, rows_dev)), ("seq", "emb"), 0, 0, tiled=True
        )
        everyone = jnp.pad(everyone, ((edge, edge), (0, 0)))
        mine = lax.dynamic_slice_in_dim(everyone, start, 2 * slots, 0).reshape(slots, 2, rows_dev)
        first, second = mine[:, 0], mine[:, 1]
        own_s = jnp.where(core == 0, first, second)
        peer_s = jnp.where(core == 0, second, first)
        cols = jnp.concatenate([to_slot_order(own_s), to_slot_order(peer_s)]).reshape(-1)
        return jnp.where(valid, cols, 0.0)

    scaling = valid.astype(jnp.float32)
    inverse = jnp.zeros((rows_dev,), jnp.float32)
    kern = kernel()
    for step in range(ITERS):
        inverse = 1.0 / jnp.sum(kern * scaling[None, :], axis=1)
        part = jnp.sum(kern * inverse[:, None], axis=0)
        scaling = column_scaling(part)
    totals = jnp.sum(kern * scaling[None, :], axis=1)
    row_mass = inverse * totals
    weights = (kern * scaling[None, :] / totals[:, None]).astype(jnp.bfloat16)
    all_groups = own_groups + peer_groups
    edges = [0]
    for g in all_groups:
        edges.append(edges[-1] + g.shape[0])
    mixed = sum(
        jnp.dot(weights[:, edges[k] : edges[k + 1]], g, preferred_element_type=jnp.float32)
        for k, g in enumerate(all_groups)
    ).astype(jnp.bfloat16)
    projected = lax.all_to_all(mixed, "emb", split_axis=1, concat_axis=0, tiled=True)
    return (projected, row_mass)


def solution(mesh):
    in_specs = (P("seq", "emb"), P("seq", "emb"), P(), P(("seq", "emb")))
    out_specs = (P("seq", "emb"), P(("seq", "emb")))
    return jax.shard_map(
        per_device, mesh=mesh, in_specs=in_specs, out_specs=out_specs, check_vma=False
    )
```

```python
import jax
import jax.numpy as jnp
from jax import lax
from jax.sharding import PartitionSpec as P

BAND = 2048
OFFSET_BLOCK = 64
ITERS = 3


INV_EPS = 50.0
PENALTY = 0.04


def shifted_2(block, axis, distance):
    devices = range(lax.axis_size(axis))
    route = [(i - distance, i) for i in devices if i - distance in devices]
    return lax.ppermute(block, axis, route)


def per_device(source, target, doc_ids, offsets):
    n_emb = lax.axis_size("emb")
    rows_dev = source.shape[0] // n_emb
    place = lax.axis_index(("seq", "emb"))
    sentences = doc_ids.shape[0]
    reach = 2 * BAND
    hops = reach // rows_dev
    width = rows_dev + 2 * reach
    tgt_rows = lax.all_to_all(target, "emb", split_axis=0, concat_axis=1, tiled=True)
    src_rows = lax.all_to_all(source, "emb", split_axis=0, concat_axis=1, tiled=True)
    half = hops // 2
    core = place % 2
    n_emb_axis = lax.axis_size("emb")
    emb_here = lax.axis_index("emb")
    reach_blocks = -(-(half * 2 + n_emb_axis - 1) // n_emb_axis) - 1
    stacked = jnp.stack(
        [
            tgt_rows if q == 0 else shifted_2(tgt_rows, "seq", -q)
            for q in range(-reach_blocks, reach_blocks + 1)
        ]
    )
    src_rows, stacked = lax.optimization_barrier((src_rows, stacked))
    pieces = []
    order = []
    for e in range(0, n_emb_axis, 2):
        wanted = [m for m in range(-half, half + 1) if (2 * m - e) % n_emb_axis == 0]
        order += wanted
        if e == 0:
            pieces.append(stacked)
            continue
        dest = (emb_here - e) % n_emb_axis
        picks = [
            lax.dynamic_index_in_dim(
                stacked, (dest + 2 * m) // n_emb_axis + reach_blocks, 0, keepdims=False
            )
            for m in wanted
        ]
        pieces.append(
            lax.ppermute(
                jnp.stack(picks),
                "emb",
                [(src, (src - e) % n_emb_axis) for src in range(n_emb_axis)],
            )
        )
    own = jnp.concatenate(pieces, axis=0).reshape(-1, tgt_rows.shape[-1])
    rank = {m: k for k, m in enumerate(order)}

    def to_m_order(rows):
        return jnp.stack([rows[rank[m]] for m in range(-half, half + 1)])

    def to_slot_order(rows):
        return jnp.stack([rows[m + half] for m in order])

    peer = lax.ppermute(own, "emb", [(e, e ^ 1) for e in range(n_emb_axis)])
    slots = 2 * half + 1
    lag = 2 * jnp.asarray(order, dtype=jnp.int32)
    slot_chunk = jnp.concatenate([place + lag, place + (1 - 2 * core) + lag])
    src_scale = lax.rsqrt(jnp.sum(jnp.square(src_rows.astype(jnp.float32)), axis=1) + 1e-06)
    own_scale = lax.rsqrt(jnp.sum(jnp.square(own.astype(jnp.float32)), axis=1) + 1e-06)
    peer_scale = lax.ppermute(own_scale, "emb", [(e, e ^ 1) for e in range(n_emb_axis)])
    first_row = place * rows_dev
    src_pos = first_row + jnp.arange(rows_dev, dtype=jnp.int32)
    tgt_pos = (slot_chunk[:, None] * rows_dev + jnp.arange(rows_dev, dtype=jnp.int32)[None, :]).reshape(-1)
    valid = (tgt_pos >= 0) & (tgt_pos < sentences)
    shifted = jnp.repeat(offsets, OFFSET_BLOCK)
    band = (jnp.abs(tgt_pos[None, :] - src_pos[:, None] - shifted[:, None]) <= BAND) & valid[
        None, :
    ]
    pad_docs = jnp.pad(doc_ids, (reach + rows_dev, reach + rows_dev), constant_values=-1)
    natural = lax.dynamic_slice_in_dim(pad_docs, first_row, (2 * slots + 1) * rows_dev, 0)
    natural = natural.reshape(2 * slots + 1, rows_dev)
    own_docs = to_slot_order(natural[1::2])
    peer_docs = to_slot_order(jnp.where(core == 0, natural[2::2], natural[0 : 2 * slots : 2]))
    tgt_docs = jnp.concatenate([own_docs, peer_docs]).reshape(-1)
    same = (
        lax.dynamic_slice_in_dim(doc_ids, first_row, rows_dev, 0)[:, None] == tgt_docs[None, :]
    )
    penalty = jnp.where(same, 0.0, PENALTY)

    def cosines():
        def part(block, scale):
            dots = lax.dot_general(
                src_rows, block, (((1,), (1,)), ((), ())), preferred_element_type=jnp.float32
            )
            return dots * src_scale[:, None] * scale[None, :]

        return jnp.concatenate([part(own, own_scale), part(peer, peer_scale)], axis=1)

    def to_kernel(cosine):
        return jnp.where(band, jnp.exp((cosine - penalty) * INV_EPS), 0.0)

    def kernel():
        return to_kernel(cosines())

    n_dev = lax.axis_size(("seq", "emb"))
    edge = slots

    def column_scaling(part):
        own_p, peer_p = part.reshape(2, slots, rows_dev)
        own_p, peer_p = to_m_order(own_p), to_m_order(peer_p)
        first = jnp.where(core == 0, own_p, peer_p)
        second = jnp.where(core == 0, peer_p, own_p)
        woven = jnp.stack([first, second], axis=1).reshape(2 * slots, rows_dev)
        start = place - 2 * half - core + edge
        spread = lax.dynamic_update_slice_in_dim(
            jnp.zeros((n_dev + 2 * edge, rows_dev), jnp.float32), woven, start, 0
        )
        to_owner = lax.all_to_all(spread[edge : edge + n_dev], ("seq", "emb"), 0, 0, tiled=True)
        own_scaling = 1.0 / jnp.sum(to_owner, axis=0)
        everyone = lax.all_to_all(
            jnp.broadcast_to(own_scaling[None, :], (n_dev, rows_dev)), ("seq", "emb"), 0, 0, tiled=True
        )
        everyone = jnp.pad(everyone, ((edge, edge), (0, 0)))
        mine = lax.dynamic_slice_in_dim(everyone, start, 2 * slots, 0).reshape(slots, 2, rows_dev)
        first, second = mine[:, 0], mine[:, 1]
        own_s = jnp.where(core == 0, first, second)
        peer_s = jnp.where(core == 0, second, first)
        cols = jnp.concatenate([to_slot_order(own_s), to_slot_order(peer_s)]).reshape(-1)
        return jnp.where(valid, cols, 0.0)

    scaling = valid.astype(jnp.float32)
    inverse = jnp.zeros((rows_dev,), jnp.float32)
    kern = kernel()
    for step in range(ITERS):
        inverse = 1.0 / jnp.sum(kern * scaling[None, :], axis=1)
        part = jnp.sum(kern * inverse[:, None], axis=0)
        scaling = column_scaling(part)
    totals = jnp.sum(kern * scaling[None, :], axis=1)
    row_mass = inverse * totals
    weights = (kern * scaling[None, :] / totals[:, None]).astype(jnp.bfloat16)
    split = own.shape[0]
    mixed = (
        jnp.dot(weights[:, :split], own, preferred_element_type=jnp.float32)
        + jnp.dot(weights[:, split:], peer, preferred_element_type=jnp.float32)
    ).astype(jnp.bfloat16)
    projected = lax.all_to_all(mixed, "emb", split_axis=1, concat_axis=0, tiled=True)
    return (projected, row_mass)


def solution(mesh):
    in_specs = (P("seq", "emb"), P("seq", "emb"), P(), P(("seq", "emb")))
    out_specs = (P("seq", "emb"), P(("seq", "emb")))
    return jax.shard_map(
        per_device, mesh=mesh, in_specs=in_specs, out_specs=out_specs, check_vma=False
    )
```

```python
import jax
import jax.numpy as jnp
from jax import lax
from jax.sharding import PartitionSpec as P

BAND = 2048
OFFSET_BLOCK = 64
ITERS = 3


INV_EPS = 50.0
PENALTY = 0.04


def shifted_2(block, axis, distance):
    devices = range(lax.axis_size(axis))
    route = [(i - distance, i) for i in devices if i - distance in devices]
    return lax.ppermute(block, axis, route)


def per_device(source, target, doc_ids, offsets):
    n_emb = lax.axis_size("emb")
    rows_dev = source.shape[0] // n_emb
    place = lax.axis_index(("seq", "emb"))
    sentences = doc_ids.shape[0]
    reach = 2 * BAND
    hops = reach // rows_dev
    width = rows_dev + 2 * reach
    tgt_rows = lax.all_to_all(target, "emb", split_axis=0, concat_axis=1, tiled=True)
    src_rows = lax.all_to_all(source, "emb", split_axis=0, concat_axis=1, tiled=True)
    half = hops // 2
    core = place % 2
    n_emb_axis = lax.axis_size("emb")
    emb_here = lax.axis_index("emb")
    reach_blocks = -(-(half * 2 + n_emb_axis - 1) // n_emb_axis) - 1
    stacked = jnp.stack(
        [
            tgt_rows if q == 0 else shifted_2(tgt_rows, "seq", -q)
            for q in range(-reach_blocks, reach_blocks + 1)
        ]
    )
    src_rows, stacked = lax.optimization_barrier((src_rows, stacked))
    by_m = {}
    for e in range(0, n_emb_axis, 2):
        wanted = [m for m in range(-half, half + 1) if (2 * m - e) % n_emb_axis == 0]
        if e == 0:
            for m in wanted:
                by_m[m] = stacked[(2 * m) // n_emb_axis + reach_blocks]
            continue
        dest = (emb_here - e) % n_emb_axis
        picks = [
            lax.dynamic_index_in_dim(
                stacked, (dest + 2 * m) // n_emb_axis + reach_blocks, 0, keepdims=False
            )
            for m in wanted
        ]
        moved = lax.ppermute(
            jnp.stack(picks),
            "emb",
            [(src, (src - e) % n_emb_axis) for src in range(n_emb_axis)],
        )
        for k, m in enumerate(wanted):
            by_m[m] = moved[k]
    own = jnp.zeros(((2 * half + 1) * rows_dev, tgt_rows.shape[-1]), tgt_rows.dtype)
    for m in sorted(by_m, key=lambda m: (2 * m) % n_emb_axis != 0):
        own = lax.dynamic_update_slice_in_dim(own, by_m[m], (m + half) * rows_dev, 0)
    peer = lax.ppermute(own, "emb", [(e, e ^ 1) for e in range(n_emb_axis)])
    slots = 2 * half + 1
    lag = 2 * (jnp.arange(slots, dtype=jnp.int32) - half)
    slot_chunk = jnp.concatenate([place + lag, place + (1 - 2 * core) + lag])
    src_scale = lax.rsqrt(jnp.sum(jnp.square(src_rows.astype(jnp.float32)), axis=1) + 1e-06)
    own_scale = lax.rsqrt(jnp.sum(jnp.square(own.astype(jnp.float32)), axis=1) + 1e-06)
    peer_scale = lax.ppermute(own_scale, "emb", [(e, e ^ 1) for e in range(n_emb_axis)])
    first_row = place * rows_dev
    src_pos = first_row + jnp.arange(rows_dev, dtype=jnp.int32)
    tgt_pos = (slot_chunk[:, None] * rows_dev + jnp.arange(rows_dev, dtype=jnp.int32)[None, :]).reshape(-1)
    valid = (tgt_pos >= 0) & (tgt_pos < sentences)
    shifted = jnp.repeat(offsets, OFFSET_BLOCK)
    band = (jnp.abs(tgt_pos[None, :] - src_pos[:, None] - shifted[:, None]) <= BAND) & valid[
        None, :
    ]
    pad_docs = jnp.pad(doc_ids, (reach + rows_dev, reach + rows_dev), constant_values=-1)
    natural = lax.dynamic_slice_in_dim(pad_docs, first_row, (2 * slots + 1) * rows_dev, 0)
    natural = natural.reshape(2 * slots + 1, rows_dev)
    own_docs = natural[1::2]
    peer_docs = jnp.where(core == 0, natural[2::2], natural[0 : 2 * slots : 2])
    tgt_docs = jnp.concatenate([own_docs, peer_docs]).reshape(-1)
    same = (
        lax.dynamic_slice_in_dim(doc_ids, first_row, rows_dev, 0)[:, None] == tgt_docs[None, :]
    )
    penalty = jnp.where(same, 0.0, PENALTY)

    def cosines():
        def part(block, scale):
            dots = lax.dot_general(
                src_rows, block, (((1,), (1,)), ((), ())), preferred_element_type=jnp.float32
            )
            return dots * src_scale[:, None] * scale[None, :]

        return jnp.concatenate([part(own, own_scale), part(peer, peer_scale)], axis=1)

    def to_kernel(cosine):
        return jnp.where(band, jnp.exp((cosine - penalty) * INV_EPS), 0.0)

    def kernel():
        return to_kernel(cosines())

    n_dev = lax.axis_size(("seq", "emb"))
    edge = slots

    def column_scaling(part):
        own_p, peer_p = part.reshape(2, slots, rows_dev)
        first = jnp.where(core == 0, own_p, peer_p)
        second = jnp.where(core == 0, peer_p, own_p)
        woven = jnp.stack([first, second], axis=1).reshape(2 * slots, rows_dev)
        start = place - 2 * half - core + edge
        spread = lax.dynamic_update_slice_in_dim(
            jnp.zeros((n_dev + 2 * edge, rows_dev), jnp.float32), woven, start, 0
        )
        to_owner = lax.all_to_all(spread[edge : edge + n_dev], ("seq", "emb"), 0, 0, tiled=True)
        own_scaling = 1.0 / jnp.sum(to_owner, axis=0)
        everyone = lax.all_to_all(
            jnp.broadcast_to(own_scaling[None, :], (n_dev, rows_dev)), ("seq", "emb"), 0, 0, tiled=True
        )
        everyone = jnp.pad(everyone, ((edge, edge), (0, 0)))
        mine = lax.dynamic_slice_in_dim(everyone, start, 2 * slots, 0).reshape(slots, 2, rows_dev)
        first, second = mine[:, 0], mine[:, 1]
        own_s = jnp.where(core == 0, first, second)
        peer_s = jnp.where(core == 0, second, first)
        cols = jnp.concatenate([own_s, peer_s]).reshape(-1)
        return jnp.where(valid, cols, 0.0)

    scaling = valid.astype(jnp.float32)
    inverse = jnp.zeros((rows_dev,), jnp.float32)
    kern = kernel()
    for step in range(ITERS):
        inverse = 1.0 / jnp.sum(kern * scaling[None, :], axis=1)
        part = jnp.sum(kern * inverse[:, None], axis=0)
        scaling = column_scaling(part)
    totals = jnp.sum(kern * scaling[None, :], axis=1)
    row_mass = inverse * totals
    weights = (kern * scaling[None, :] / totals[:, None]).astype(jnp.bfloat16)
    split = own.shape[0]
    mixed = (
        jnp.dot(weights[:, :split], own, preferred_element_type=jnp.float32)
        + jnp.dot(weights[:, split:], peer, preferred_element_type=jnp.float32)
    ).astype(jnp.bfloat16)
    projected = lax.all_to_all(mixed, "emb", split_axis=1, concat_axis=0, tiled=True)
    return (projected, row_mass)


def solution(mesh):
    in_specs = (P("seq", "emb"), P("seq", "emb"), P(), P(("seq", "emb")))
    out_specs = (P("seq", "emb"), P(("seq", "emb")))
    return jax.shard_map(
        per_device, mesh=mesh, in_specs=in_specs, out_specs=out_specs, check_vma=False
    )
```

```python
import jax
import jax.numpy as jnp
from jax import lax
from jax.sharding import PartitionSpec as P

BAND = 2048
OFFSET_BLOCK = 64
ITERS = 3


INV_EPS = 50.0
PENALTY = 0.04


def shifted_2(block, axis, distance):
    devices = range(lax.axis_size(axis))
    route = [(i - distance, i) for i in devices if i - distance in devices]
    return lax.ppermute(block, axis, route)


def per_device(source, target, doc_ids, offsets):
    n_emb = lax.axis_size("emb")
    rows_dev = source.shape[0] // n_emb
    place = lax.axis_index(("seq", "emb"))
    sentences = doc_ids.shape[0]
    reach = 2 * BAND
    hops = reach // rows_dev
    width = rows_dev + 2 * reach
    tgt_rows = lax.all_to_all(target, "emb", split_axis=0, concat_axis=1, tiled=True)
    src_rows = lax.all_to_all(source, "emb", split_axis=0, concat_axis=1, tiled=True)
    half = hops // 2
    core = place % 2
    n_emb_axis = lax.axis_size("emb")
    emb_here = lax.axis_index("emb")
    reach_blocks = -(-(half * 2 + n_emb_axis - 1) // n_emb_axis) - 1
    stacked = jnp.stack(
        [
            tgt_rows if q == 0 else shifted_2(tgt_rows, "seq", -q)
            for q in range(-reach_blocks, reach_blocks + 1)
        ]
    )
    src_rows, stacked = lax.optimization_barrier((src_rows, stacked))
    by_m = {}
    for e in sorted(range(0, n_emb_axis, 2), key=lambda e: -min(e, n_emb_axis - e)):
        wanted = [m for m in range(-half, half + 1) if (2 * m - e) % n_emb_axis == 0]
        if e == 0:
            for m in wanted:
                by_m[m] = stacked[(2 * m) // n_emb_axis + reach_blocks]
            continue
        dest = (emb_here - e) % n_emb_axis
        picks = [
            lax.dynamic_index_in_dim(
                stacked, (dest + 2 * m) // n_emb_axis + reach_blocks, 0, keepdims=False
            )
            for m in wanted
        ]
        moved = lax.ppermute(
            jnp.stack(picks),
            "emb",
            [(src, (src - e) % n_emb_axis) for src in range(n_emb_axis)],
        )
        for k, m in enumerate(wanted):
            by_m[m] = moved[k]
    own = jnp.zeros(((2 * half + 1) * rows_dev, tgt_rows.shape[-1]), tgt_rows.dtype)
    for m in sorted(by_m, key=lambda m: (2 * m) % n_emb_axis != 0):
        own = lax.dynamic_update_slice_in_dim(own, by_m[m], (m + half) * rows_dev, 0)
    peer = lax.ppermute(own, "emb", [(e, e ^ 1) for e in range(n_emb_axis)])
    slots = 2 * half + 1
    lag = 2 * (jnp.arange(slots, dtype=jnp.int32) - half)
    slot_chunk = jnp.concatenate([place + lag, place + (1 - 2 * core) + lag])
    src_scale = lax.rsqrt(jnp.sum(jnp.square(src_rows.astype(jnp.float32)), axis=1) + 1e-06)
    own_scale = lax.rsqrt(jnp.sum(jnp.square(own.astype(jnp.float32)), axis=1) + 1e-06)
    peer_scale = lax.ppermute(own_scale, "emb", [(e, e ^ 1) for e in range(n_emb_axis)])
    first_row = place * rows_dev
    src_pos = first_row + jnp.arange(rows_dev, dtype=jnp.int32)
    tgt_pos = (slot_chunk[:, None] * rows_dev + jnp.arange(rows_dev, dtype=jnp.int32)[None, :]).reshape(-1)
    valid = (tgt_pos >= 0) & (tgt_pos < sentences)
    shifted = jnp.repeat(offsets, OFFSET_BLOCK)
    band = (jnp.abs(tgt_pos[None, :] - src_pos[:, None] - shifted[:, None]) <= BAND) & valid[
        None, :
    ]
    pad_docs = jnp.pad(doc_ids, (reach + rows_dev, reach + rows_dev), constant_values=-1)
    natural = lax.dynamic_slice_in_dim(pad_docs, first_row, (2 * slots + 1) * rows_dev, 0)
    natural = natural.reshape(2 * slots + 1, rows_dev)
    own_docs = natural[1::2]
    peer_docs = jnp.where(core == 0, natural[2::2], natural[0 : 2 * slots : 2])
    tgt_docs = jnp.concatenate([own_docs, peer_docs]).reshape(-1)
    same = (
        lax.dynamic_slice_in_dim(doc_ids, first_row, rows_dev, 0)[:, None] == tgt_docs[None, :]
    )
    penalty = jnp.where(same, 0.0, PENALTY)

    def cosines():
        def part(block, scale):
            dots = lax.dot_general(
                src_rows, block, (((1,), (1,)), ((), ())), preferred_element_type=jnp.float32
            )
            return dots * src_scale[:, None] * scale[None, :]

        return jnp.concatenate([part(own, own_scale), part(peer, peer_scale)], axis=1)

    def to_kernel(cosine):
        return jnp.where(band, jnp.exp((cosine - penalty) * INV_EPS), 0.0)

    def kernel():
        return to_kernel(cosines())

    n_dev = lax.axis_size(("seq", "emb"))
    edge = slots

    def column_scaling(part):
        own_p, peer_p = part.reshape(2, slots, rows_dev)
        first = jnp.where(core == 0, own_p, peer_p)
        second = jnp.where(core == 0, peer_p, own_p)
        woven = jnp.stack([first, second], axis=1).reshape(2 * slots, rows_dev)
        start = place - 2 * half - core + edge
        spread = lax.dynamic_update_slice_in_dim(
            jnp.zeros((n_dev + 2 * edge, rows_dev), jnp.float32), woven, start, 0
        )
        to_owner = lax.all_to_all(spread[edge : edge + n_dev], ("seq", "emb"), 0, 0, tiled=True)
        own_scaling = 1.0 / jnp.sum(to_owner, axis=0)
        everyone = lax.all_to_all(
            jnp.broadcast_to(own_scaling[None, :], (n_dev, rows_dev)), ("seq", "emb"), 0, 0, tiled=True
        )
        everyone = jnp.pad(everyone, ((edge, edge), (0, 0)))
        mine = lax.dynamic_slice_in_dim(everyone, start, 2 * slots, 0).reshape(slots, 2, rows_dev)
        first, second = mine[:, 0], mine[:, 1]
        own_s = jnp.where(core == 0, first, second)
        peer_s = jnp.where(core == 0, second, first)
        cols = jnp.concatenate([own_s, peer_s]).reshape(-1)
        return jnp.where(valid, cols, 0.0)

    scaling = valid.astype(jnp.float32)
    inverse = jnp.zeros((rows_dev,), jnp.float32)
    kern = kernel()
    for step in range(ITERS):
        inverse = 1.0 / jnp.sum(kern * scaling[None, :], axis=1)
        part = jnp.sum(kern * inverse[:, None], axis=0)
        scaling = column_scaling(part)
    totals = jnp.sum(kern * scaling[None, :], axis=1)
    row_mass = inverse * totals
    weights = (kern * scaling[None, :] / totals[:, None]).astype(jnp.bfloat16)
    split = own.shape[0]
    mixed = (
        jnp.dot(weights[:, :split], own, preferred_element_type=jnp.float32)
        + jnp.dot(weights[:, split:], peer, preferred_element_type=jnp.float32)
    ).astype(jnp.bfloat16)
    projected = lax.all_to_all(mixed, "emb", split_axis=1, concat_axis=0, tiled=True)
    return (projected, row_mass)


def solution(mesh):
    in_specs = (P("seq", "emb"), P("seq", "emb"), P(), P(("seq", "emb")))
    out_specs = (P("seq", "emb"), P(("seq", "emb")))
    return jax.shard_map(
        per_device, mesh=mesh, in_specs=in_specs, out_specs=out_specs, check_vma=False
    )
```

```python
import jax
import jax.numpy as jnp
from jax import lax
from jax.sharding import PartitionSpec as P

BAND = 2048
OFFSET_BLOCK = 64
ITERS = 3


INV_EPS = 50.0
PENALTY = 0.04


def shifted_2(block, axis, distance):
    devices = range(lax.axis_size(axis))
    route = [(i - distance, i) for i in devices if i - distance in devices]
    return lax.ppermute(block, axis, route)


def per_device(source, target, doc_ids, offsets):
    n_emb = lax.axis_size("emb")
    rows_dev = source.shape[0] // n_emb
    place = lax.axis_index(("seq", "emb"))
    sentences = doc_ids.shape[0]
    reach = 2 * BAND
    hops = reach // rows_dev
    width = rows_dev + 2 * reach
    tgt_rows = lax.all_to_all(target, "emb", split_axis=0, concat_axis=1, tiled=True)
    src_rows = lax.all_to_all(source, "emb", split_axis=0, concat_axis=1, tiled=True)
    half = hops // 2
    core = place % 2
    n_emb_axis = lax.axis_size("emb")
    emb_here = lax.axis_index("emb")
    reach_blocks = -(-(half * 2 + n_emb_axis - 1) // n_emb_axis) - 1
    stacked = jnp.stack(
        [
            tgt_rows if q == 0 else shifted_2(tgt_rows, "seq", -q)
            for q in range(-reach_blocks, reach_blocks + 1)
        ]
    )
    src_rows, stacked = lax.optimization_barrier((src_rows, stacked))
    by_m = {}
    for e in sorted(range(0, n_emb_axis, 2), key=lambda e: (-min(e, n_emb_axis - e), -e)):
        wanted = [m for m in range(-half, half + 1) if (2 * m - e) % n_emb_axis == 0]
        if e == 0:
            for m in wanted:
                by_m[m] = stacked[(2 * m) // n_emb_axis + reach_blocks]
            continue
        dest = (emb_here - e) % n_emb_axis
        picks = [
            lax.dynamic_index_in_dim(
                stacked, (dest + 2 * m) // n_emb_axis + reach_blocks, 0, keepdims=False
            )
            for m in wanted
        ]
        moved = lax.ppermute(
            jnp.stack(picks),
            "emb",
            [(src, (src - e) % n_emb_axis) for src in range(n_emb_axis)],
        )
        for k, m in enumerate(wanted):
            by_m[m] = moved[k]
    own = jnp.zeros(((2 * half + 1) * rows_dev, tgt_rows.shape[-1]), tgt_rows.dtype)
    for m in sorted(by_m, key=lambda m: (2 * m) % n_emb_axis != 0):
        own = lax.dynamic_update_slice_in_dim(own, by_m[m], (m + half) * rows_dev, 0)
    peer = lax.ppermute(own, "emb", [(e, e ^ 1) for e in range(n_emb_axis)])
    slots = 2 * half + 1
    lag = 2 * (jnp.arange(slots, dtype=jnp.int32) - half)
    slot_chunk = jnp.concatenate([place + lag, place + (1 - 2 * core) + lag])
    src_scale = lax.rsqrt(jnp.sum(jnp.square(src_rows.astype(jnp.float32)), axis=1) + 1e-06)
    own_scale = lax.rsqrt(jnp.sum(jnp.square(own.astype(jnp.float32)), axis=1) + 1e-06)
    peer_scale = lax.ppermute(own_scale, "emb", [(e, e ^ 1) for e in range(n_emb_axis)])
    first_row = place * rows_dev
    src_pos = first_row + jnp.arange(rows_dev, dtype=jnp.int32)
    tgt_pos = (slot_chunk[:, None] * rows_dev + jnp.arange(rows_dev, dtype=jnp.int32)[None, :]).reshape(-1)
    valid = (tgt_pos >= 0) & (tgt_pos < sentences)
    shifted = jnp.repeat(offsets, OFFSET_BLOCK)
    band = (jnp.abs(tgt_pos[None, :] - src_pos[:, None] - shifted[:, None]) <= BAND) & valid[
        None, :
    ]
    pad_docs = jnp.pad(doc_ids, (reach + rows_dev, reach + rows_dev), constant_values=-1)
    natural = lax.dynamic_slice_in_dim(pad_docs, first_row, (2 * slots + 1) * rows_dev, 0)
    natural = natural.reshape(2 * slots + 1, rows_dev)
    own_docs = natural[1::2]
    peer_docs = jnp.where(core == 0, natural[2::2], natural[0 : 2 * slots : 2])
    tgt_docs = jnp.concatenate([own_docs, peer_docs]).reshape(-1)
    same = (
        lax.dynamic_slice_in_dim(doc_ids, first_row, rows_dev, 0)[:, None] == tgt_docs[None, :]
    )
    penalty = jnp.where(same, 0.0, PENALTY)

    def cosines():
        def part(block, scale):
            dots = lax.dot_general(
                src_rows, block, (((1,), (1,)), ((), ())), preferred_element_type=jnp.float32
            )
            return dots * src_scale[:, None] * scale[None, :]

        return jnp.concatenate([part(own, own_scale), part(peer, peer_scale)], axis=1)

    def to_kernel(cosine):
        return jnp.where(band, jnp.exp((cosine - penalty) * INV_EPS), 0.0)

    def kernel():
        return to_kernel(cosines())

    n_dev = lax.axis_size(("seq", "emb"))
    edge = slots

    def column_scaling(part):
        own_p, peer_p = part.reshape(2, slots, rows_dev)
        first = jnp.where(core == 0, own_p, peer_p)
        second = jnp.where(core == 0, peer_p, own_p)
        woven = jnp.stack([first, second], axis=1).reshape(2 * slots, rows_dev)
        start = place - 2 * half - core + edge
        spread = lax.dynamic_update_slice_in_dim(
            jnp.zeros((n_dev + 2 * edge, rows_dev), jnp.float32), woven, start, 0
        )
        to_owner = lax.all_to_all(spread[edge : edge + n_dev], ("seq", "emb"), 0, 0, tiled=True)
        own_scaling = 1.0 / jnp.sum(to_owner, axis=0)
        everyone = lax.all_to_all(
            jnp.broadcast_to(own_scaling[None, :], (n_dev, rows_dev)), ("seq", "emb"), 0, 0, tiled=True
        )
        everyone = jnp.pad(everyone, ((edge, edge), (0, 0)))
        mine = lax.dynamic_slice_in_dim(everyone, start, 2 * slots, 0).reshape(slots, 2, rows_dev)
        first, second = mine[:, 0], mine[:, 1]
        own_s = jnp.where(core == 0, first, second)
        peer_s = jnp.where(core == 0, second, first)
        cols = jnp.concatenate([own_s, peer_s]).reshape(-1)
        return jnp.where(valid, cols, 0.0)

    scaling = valid.astype(jnp.float32)
    inverse = jnp.zeros((rows_dev,), jnp.float32)
    kern = kernel()
    for step in range(ITERS):
        inverse = 1.0 / jnp.sum(kern * scaling[None, :], axis=1)
        part = jnp.sum(kern * inverse[:, None], axis=0)
        scaling = column_scaling(part)
    totals = jnp.sum(kern * scaling[None, :], axis=1)
    row_mass = inverse * totals
    weights = (kern * scaling[None, :] / totals[:, None]).astype(jnp.bfloat16)
    split = own.shape[0]
    mixed = (
        jnp.dot(weights[:, :split], own, preferred_element_type=jnp.float32)
        + jnp.dot(weights[:, split:], peer, preferred_element_type=jnp.float32)
    ).astype(jnp.bfloat16)
    projected = lax.all_to_all(mixed, "emb", split_axis=1, concat_axis=0, tiled=True)
    return (projected, row_mass)


def solution(mesh):
    in_specs = (P("seq", "emb"), P("seq", "emb"), P(), P(("seq", "emb")))
    out_specs = (P("seq", "emb"), P(("seq", "emb")))
    return jax.shard_map(
        per_device, mesh=mesh, in_specs=in_specs, out_specs=out_specs, check_vma=False
    )
```
